32 devices in a mesh: groups: 2 (over y), ctx: 8 (over z, x), tensor: 2 (over core).
Axes of the slice: x: 2, y: 2, z: 4, core: 2. Of those that a mesh axis runs over, the one named last changes fastest.
Arguments:
- light_query: bfloat16 [2048, 4096], P(('groups', 'ctx'), 'tensor'), parts along dimension 0, may hold values from -6 to 6
- light_key: bfloat16 [2048, 4096], P(('groups', 'ctx'), 'tensor'), parts along dimension 0, may hold values from -6 to 6
- light_value: bfloat16 [2048, 4096], P(('groups', 'ctx'), 'tensor'), parts along dimension 0, may hold values from -500 to 500
- light_gate: bfloat16 [2048, 4096], P(('groups', 'ctx'), 'tensor'), parts along dimension 0, may hold values from -6 to 6
- log_decay: float32 [32, 2048], P('tensor', ('groups', 'ctx')), parts along dimension 1, may hold values from -2.2 to 0
- norm_gain: float32 [4096], P('tensor'), may hold values from 0.1 to 1.9
- soft_query: bfloat16 [2048, 4096], P(('groups', 'ctx'), 'tensor'), parts along dimension 0, may hold values from -9 to 9
- soft_key: bfloat16 [2048, 512], P(('groups', 'ctx'), 'tensor'), parts along dimension 0, may hold values from -9 to 9
- soft_value: bfloat16 [2048, 512], P(('groups', 'ctx'), 'tensor'), parts along dimension 0, may hold values from -6 to 6
- segment_ids: int32 [2048], P(('groups', 'ctx')), parts along dimension 0, may hold values from 0 to 3, never falling along the last dimension, each value on 1 to 512 neighbouring positions
Outputs:
- light_out: bfloat16 [2048, 4096], P(('groups', 'ctx'), 'tensor'), parts along dimension 0
- soft_out: bfloat16 [2048, 4096], P(('groups', 'ctx'), 'tensor'), parts along dimension 0
The draws below stay inside these ranges and needn't reach their ends.
There are 2 independent parts, one for each index of `groups`. The reference program is written for one: setup_inputs(seed, part) draws one part's arguments, and reference() takes and returns one part's arrays. A program takes and returns all parts, laid end to end along the dimension named above; an argument that names none is the same for every part. Nothing has to cross between parts.
Inputs may be any that keep to these rules, and one draw needn't show every extreme that they name: `segment_ids`: segment ids never fall along the slab; every prompt covers 1 to 512 consecutive positions and some prompt covers exactly 512.
All inputs are finite; a program needn't handle non-finite values.
Results may differ from the reference program's by a relative error of at most 0.007.
Values may be sent and summed in bfloat16 or wider, within the bound.
No kernel may reach another device: no remote copies, remote signals or barrier semaphores. Data moves between devices by JAX's collectives and lax.ppermute only.
A program may use at most 256 MiB of HBM per device.

```python
import math
import jax
import jax.numpy as jnp
import numpy as np
from jax import lax

HEADS = 32
KV_HEADS = 4
HD = 128
TOK_DEV = 128
PACKED_LENGTH = 1024
MAXDOC = 512
DOCS = 4


def draw_light_value(key, part):
    columns = HEADS * HD
    key_base = jax.random.fold_in(key, 21)
    key_row = jax.random.fold_in(key, 22)
    head_index = (jnp.arange(columns) // HD).astype(jnp.float32)
    column_scale = jnp.exp(math.log(10.0) * head_index / max(HEADS - 1, 1))
    row_scale = jnp.exp(jax.random.uniform(key_row, (PACKED_LENGTH, 1), minval=0.0, maxval=math.log(10.0)))
    base = jnp.clip(jax.random.normal(key_base, (PACKED_LENGTH, columns)), -5.0, 5.0)
    return (base * column_scale[None, :] * row_scale).astype(jnp.bfloat16)


def draw_log_decay(key, part):
    slow_share = 0.5
    slow_heads = jax.random.bernoulli(jax.random.fold_in(key, 31), slow_share, (HEADS, 1))
    fast_rate = jnp.exp(jax.random.uniform(jax.random.fold_in(key, 32), (HEADS, 1), minval=math.log(1.0 / 50.0), maxval=math.log(1.0 / 30.0)))
    head_decay_rate = jnp.where(slow_heads, 0.4 / MAXDOC, fast_rate)
    block_count = PACKED_LENGTH // TOK_DEV
    block_multiplier = jnp.exp(jax.random.uniform(jax.random.fold_in(key, 33), (HEADS, block_count, 1), minval=math.log(0.5), maxval=math.log(2.0)))
    block_multiplier = jnp.broadcast_to(block_multiplier, (HEADS, block_count, TOK_DEV)).reshape(HEADS, PACKED_LENGTH)
    token_multiplier = jax.random.uniform(jax.random.fold_in(key, 34), (HEADS, PACKED_LENGTH), minval=0.5, maxval=1.5)
    spike_position = jax.random.randint(jax.random.fold_in(key, 35), (3,), 0, PACKED_LENGTH)
    spike_retention = jax.random.uniform(jax.random.fold_in(key, 36), (3,), minval=0.5, maxval=0.8)
    token_position = jnp.arange(PACKED_LENGTH)
    decay_spike = jnp.sum(jnp.where(token_position[None, :] == spike_position[:, None], jnp.log(spike_retention)[:, None], 0.0), axis=0)
    return -head_decay_rate * block_multiplier * token_multiplier + decay_spike[None, :]


def base_noise(key, columns):
    return jnp.clip(jax.random.normal(key, (PACKED_LENGTH, columns)), -5.0, 5.0)


def draw_soft_query(key, part):
    queries = base_noise(jax.random.fold_in(key, 11), HEADS * HD)
    return queries.astype(jnp.bfloat16)


def draw_soft_key(key, part):
    keys_drawn = base_noise(jax.random.fold_in(key, 12), KV_HEADS * HD)
    return keys_drawn.astype(jnp.bfloat16)


def steps_of(rng, dims, cuts, least, top_value):
    loudness = 1.0
    for axis_at, shards_of in cuts:
        heights = jax.random.uniform(jax.random.fold_in(jax.random.fold_in(rng, 6), axis_at), (shards_of,), jnp.float32, least / len(cuts), top_value / len(cuts))
        loudness = loudness * jnp.repeat(jnp.exp(heights), dims[axis_at] // shards_of).reshape((-1,) + (1,) * (len(dims) - 1 - axis_at))
    return loudness


def length_profile(amount, total, most, slope):
    weights = [(1 << 20) // math.isqrt(grade ** slope) + 1 for grade in range(2, amount + 1)]
    rest, holding = total - most - (amount - 1), [1] * (amount - 1)
    while rest > 0:
        free = [i for i in range(amount - 1) if holding[i] < most]
        pool, budget = sum([weights[i] for i in free]), rest
        for i in free:
            extra = min(most - holding[i], max(1, budget * weights[i] // pool), rest)
            holding[i] = holding[i] + extra
            rest = rest - extra
    return np.array([most] + holding)


def uneven(own_key, count, total, bound, slope):
    if count == 2:
        one = jax.random.randint(own_key, (), max(1, total - bound), min(bound, total - 1) + 1)
        return jnp.stack([one, total - one])
    sizes = jnp.asarray(length_profile(count, total, bound, slope), jnp.int32)
    couples = (count - 1) // 2
    donor, receiver = sizes[1:1 + 2 * couples:2], sizes[2:2 + 2 * couples:2]
    room = jnp.minimum(donor - 1, bound - receiver)
    passed = jax.random.randint(jax.random.fold_in(own_key, 1), (couples,), 0, 1 << 20) % (room + 1)
    sizes = sizes.at[1:1 + 2 * couples:2].set(donor - passed).at[2:2 + 2 * couples:2].set(receiver + passed)
    return sizes[jax.random.permutation(jax.random.fold_in(own_key, 2), count)]


def noise(rng, extent, spread, most, cuts=(), held_as=jnp.bfloat16):
    gain = steps_of(rng, extent, cuts, -0.22, 0.18) if cuts else 1.0
    drawn = jax.random.normal(rng, extent, jnp.float32) * spread * gain
    return jnp.minimum(jnp.maximum(drawn, -most), most).astype(held_as)


def setup_inputs(seed: int = 0, part: int = 0) -> dict:
    splits = jax.random.split(jax.random.key(seed), 11)
    part_keys = jax.random.split(jax.random.fold_in(splits[10], part), 11)
    return {
        "light_query": noise(part_keys[0], (PACKED_LENGTH, HEADS * HD), 1.0, 6.0, ((0, 8), (1, 2))),
        "light_key": noise(part_keys[1], (PACKED_LENGTH, HEADS * HD), 1.0, 6.0, ((0, 8), (1, 2))),
        "light_value": draw_light_value(jax.random.fold_in(jax.random.fold_in(splits[10], part), 71), part),
        "light_gate": noise(part_keys[3], (PACKED_LENGTH, HEADS * HD), 1.5, 6.0, ((0, 8), (1, 2))),
        "log_decay": draw_log_decay(jax.random.fold_in(jax.random.fold_in(splits[10], part), 71), part),
        "norm_gain": jnp.clip(1.0 + 0.18 * jax.random.normal(splits[5], (HEADS * HD,), jnp.float32), 0.1, 1.9),
        "soft_query": draw_soft_query(jax.random.fold_in(jax.random.fold_in(splits[10], part), 71), part),
        "soft_key": draw_soft_key(jax.random.fold_in(jax.random.fold_in(splits[10], part), 71), part),
        "soft_value": noise(part_keys[8], (PACKED_LENGTH, KV_HEADS * HD), 1.0, 6.0, ((0, 8), (1, 2))),
        "segment_ids": jnp.searchsorted(jnp.cumsum(uneven(part_keys[9], DOCS, PACKED_LENGTH, MAXDOC, 2)), jnp.arange(PACKED_LENGTH), side="right").astype(jnp.int32),
    }


NEG_BIG = -1e+30
HIGHEST = lax.Precision.HIGHEST

def light_layer(light_query, light_key, light_value, light_gate, log_decay, norm_gain, segment_ids):
    block_count = PACKED_LENGTH // TOK_DEV
    query_blocks = light_query.reshape(block_count, TOK_DEV, HEADS, HD)
    key_blocks = light_key.reshape(block_count, TOK_DEV, HEADS, HD)
    value_blocks = light_value.reshape(block_count, TOK_DEV, HEADS, HD)
    decay_blocks = log_decay.reshape(HEADS, block_count, TOK_DEV).transpose(1, 0, 2)
    seg_blocks = segment_ids.reshape(block_count, TOK_DEV)
    token_position = jnp.arange(TOK_DEV)
    causal = token_position[None, :] <= token_position[:, None]

    def advance(carry_pair, inputs):
        prior_state, prior_seg = carry_pair
        query_here, key_here, value_here, decay_here, seg_here = inputs
        query_float = query_here.astype(jnp.float32)
        value_float = value_here.astype(jnp.float32)
        decay_sum = jnp.cumsum(decay_here, axis=1)
        allowed = (seg_here[:, None] == seg_here[None, :]) & causal
        decay_gap = jnp.where(allowed[None], decay_sum[:, :, None] - decay_sum[:, None, :], -jnp.inf)
        products = jnp.einsum('thd,shd->hts', query_float, key_here.astype(jnp.float32), precision=HIGHEST)
        weights = lax.optimization_barrier((products * jnp.exp(decay_gap)).astype(jnp.bfloat16))
        mixed = jnp.einsum('hts,shd->thd', weights.astype(jnp.float32), value_float, precision=HIGHEST)
        uses_state = seg_here == prior_seg
        carried_in = jnp.einsum('thd,hde->the', query_float, prior_state, precision=HIGHEST)
        scale_in = jnp.where(uses_state[None, :], jnp.exp(decay_sum), 0.0)
        mixed = mixed + carried_in * scale_in.T[:, :, None]
        to_end = jnp.where((seg_here == seg_here[-1])[None, :], jnp.exp(decay_sum[:, -1:] - decay_sum), 0.0)
        key_weighted = lax.optimization_barrier((key_here.astype(jnp.float32) * to_end.T[:, :, None]).astype(jnp.bfloat16))
        local_state = jnp.einsum('shd,she->hde', key_weighted.astype(jnp.float32), value_float, precision=HIGHEST)
        joined = (prior_seg == seg_here[0]) & (seg_here[0] == seg_here[-1])
        carried = jnp.where(joined, jnp.exp(decay_sum[:, -1]), 0.0)
        next_state = local_state + carried[:, None, None] * prior_state
        return ((next_state, seg_here[-1]), mixed)
    start = (jnp.zeros((HEADS, HD, HD), jnp.float32), jnp.array(-1, jnp.int32))
    unused, mixed = lax.scan(advance, start, (query_blocks, key_blocks, value_blocks, decay_blocks, seg_blocks))
    mixed = mixed.reshape(PACKED_LENGTH, HEADS, HD)
    squares = lax.optimization_barrier(jnp.sum(mixed * mixed, axis=(1, 2)))
    inverse = lax.rsqrt(squares / (HEADS * HD) + 1e-06)
    gate_open = jax.nn.sigmoid(light_gate.astype(jnp.float32)).reshape(PACKED_LENGTH, HEADS, HD)
    normed = mixed * inverse[:, None, None] * norm_gain.reshape(HEADS, HD) * gate_open
    return normed.reshape(PACKED_LENGTH, HEADS * HD).astype(jnp.bfloat16)

def soft_layer(soft_query, soft_key, soft_value, segment_ids):
    group = HEADS // KV_HEADS
    block_count = PACKED_LENGTH // TOK_DEV
    key_span = MAXDOC + TOK_DEV
    padded_keys = jnp.concatenate([jnp.zeros((MAXDOC, KV_HEADS * HD), jnp.bfloat16), soft_key], axis=0)
    padded_values = jnp.concatenate([jnp.zeros((MAXDOC, KV_HEADS * HD), jnp.bfloat16), soft_value], axis=0)
    padded_seg = jnp.concatenate([jnp.full((MAXDOC,), -1, jnp.int32), segment_ids.astype(jnp.int32)], axis=0)
    key_position = jnp.arange(key_span)
    query_position = jnp.arange(TOK_DEV) + MAXDOC

    def one_block(block_index):
        start = (block_index * TOK_DEV).astype(jnp.int32)
        query_here = lax.dynamic_slice_in_dim(soft_query, start, TOK_DEV, 0).reshape(TOK_DEV, KV_HEADS, group, HD)
        key_here = lax.dynamic_slice_in_dim(padded_keys, start, key_span, 0).reshape(key_span, KV_HEADS, HD)
        value_here = lax.dynamic_slice_in_dim(padded_values, start, key_span, 0).reshape(key_span, KV_HEADS, HD)
        seg_query = lax.dynamic_slice_in_dim(segment_ids.astype(jnp.int32), start, TOK_DEV, 0)
        seg_key = lax.dynamic_slice_in_dim(padded_seg, start, key_span, 0)
        allowed = (seg_query[:, None] == seg_key[None, :]) & (key_position[None, :] <= query_position[:, None])
        scores = jnp.einsum('tkgd,skd->kgts', query_here.astype(jnp.float32), key_here.astype(jnp.float32), precision=HIGHEST) * HD ** (-0.5)
        scores = jnp.where(allowed, scores, NEG_BIG)
        row_max = lax.optimization_barrier(jnp.max(scores, axis=-1))
        prob_block = jnp.exp(scores - row_max[..., None])
        row_total = lax.optimization_barrier(jnp.sum(prob_block, axis=-1))
        rounded = lax.optimization_barrier(prob_block.astype(jnp.bfloat16))
        weighted = jnp.einsum('kgts,skd->kgtd', rounded.astype(jnp.float32), value_here.astype(jnp.float32), precision=HIGHEST)
        output = (weighted / row_total[..., None]).transpose(2, 0, 1, 3).reshape(TOK_DEV, HEADS * HD)
        return output.astype(jnp.bfloat16)
    outputs = lax.map(one_block, jnp.arange(block_count, dtype=jnp.int32))
    return outputs.reshape(PACKED_LENGTH, HEADS * HD)

def reference(light_query, light_key, light_value, light_gate, log_decay, norm_gain, soft_query, soft_key, soft_value, segment_ids):
    light_out = light_layer(light_query, light_key, light_value, light_gate, log_decay, norm_gain, segment_ids)
    soft_out = soft_layer(soft_query, soft_key, soft_value, segment_ids)
    return (light_out, soft_out)
```

```python
import jax
import jax.numpy as jnp
from jax import lax
from jax.sharding import PartitionSpec as P

NEG_BIG = -1e30
MAXDOC = 512
F32 = jnp.float32
BF16 = jnp.bfloat16


def shifted(block, axis, distance):
    devices = lax.axis_size(axis)
    route = [(i, i + distance) for i in range(devices - distance)]
    return lax.ppermute(block, axis, route)


def light_local(light_query, light_key, light_value, decay_sum, code):
    tok_rows, heads_here = light_query.shape[0], decay_sum.shape[0]
    head_size = light_query.shape[1] // heads_here
    query_heads = light_query.reshape(tok_rows, heads_here, head_size)
    key_heads = light_key.reshape(tok_rows, heads_here, head_size)
    value_heads = light_value.reshape(tok_rows, heads_here, head_size)
    token_position = jnp.arange(tok_rows)
    allowed = (code[:, None] == code[None, :]) & (token_position[None, :] <= token_position[:, None])
    decay_gap = jnp.where(allowed[None], decay_sum[:, :, None] - decay_sum[:, None, :], -jnp.inf)
    products = jnp.einsum("thd,shd->hts", query_heads, key_heads, preferred_element_type=F32)
    weights = (products * jnp.exp(decay_gap)).astype(BF16)
    mixed = jnp.einsum("hts,shd->thd", weights, value_heads, preferred_element_type=F32)
    to_end = jnp.where((code == code[-1])[None, :], jnp.exp(decay_sum[:, -1:] - decay_sum), 0.0)
    key_weighted = (key_heads * to_end.T[:, :, None]).astype(BF16)
    local_state = jnp.einsum("shd,she->hde", key_weighted, value_heads, preferred_element_type=F32)
    return mixed, local_state


def soft_window(soft_query, keys, values, code, code_window, heads_here):
    tok_rows = soft_query.shape[0]
    span = keys.shape[0]
    head_size = soft_query.shape[1] // heads_here
    kv_here = keys.shape[1] // head_size
    group = heads_here // kv_here
    queries = soft_query.reshape(tok_rows, kv_here, group, head_size)
    key_heads = keys.reshape(span, kv_here, head_size)
    value_heads = values.reshape(span, kv_here, head_size)
    key_position = jnp.arange(span)
    query_position = jnp.arange(tok_rows) + (span - tok_rows)
    allowed = (code[:, None] == code_window[None, :]) & (key_position[None, :] <= query_position[:, None])
    scores = jnp.einsum("tkgd,skd->kgts", queries, key_heads, preferred_element_type=F32) * head_size ** (-0.5)
    scores = jnp.where(allowed, scores, NEG_BIG)
    row_max = jnp.max(scores, axis=-1)
    prob_block = jnp.exp(scores - row_max[..., None])
    row_total = jnp.sum(prob_block, axis=-1)
    weighted = jnp.einsum("kgts,skd->kgtd", prob_block.astype(BF16), value_heads, preferred_element_type=F32)
    output = (weighted / row_total[..., None]).transpose(2, 0, 1, 3).reshape(tok_rows, heads_here * head_size)
    return output.astype(BF16)


def on_device(
    light_query,
    light_key,
    light_value,
    light_gate,
    log_decay,
    norm_gain,
    soft_query,
    soft_key,
    soft_value,
    segment_ids,
):
    tok_rows = light_query.shape[0]
    heads_here = log_decay.shape[0]
    head_size = light_query.shape[1] // heads_here
    kv_cols = soft_key.shape[1]
    assert -(-MAXDOC // tok_rows) == 4
    code = segment_ids.astype(F32) + 1.0
    decay_sum = jnp.cumsum(log_decay, axis=1)

    mixed, local_state = light_local(light_query, light_key, light_value, decay_sum, code)
    block_decay = jnp.exp(decay_sum[:, -1])

    soft_kv = jnp.concatenate([soft_key, soft_value], axis=1)
    meta = jnp.concatenate([code, block_decay])
    own = (local_state.astype(BF16), soft_kv, meta)
    from_1 = shifted(own, "ctx", 1)
    from_2 = shifted(own, "ctx", 2)
    state_1, kv_1, meta_1 = from_1
    state_2, kv_2, meta_2 = from_2
    code_1, decay_1 = meta_1[:tok_rows], meta_1[tok_rows:]
    code_2, decay_2 = meta_2[:tok_rows], meta_2[tok_rows:]

    link_1 = (code_2[-1] == code_1[0]) & (code_1[0] == code_1[-1])
    pair_state = state_1.astype(F32) + jnp.where(link_1, decay_1, 0.0)[:, None, None] * state_2.astype(F32)

    relay = (pair_state.astype(BF16), jnp.stack([kv_2, kv_1]), jnp.concatenate([code_2, code_1]))
    from_far = shifted(relay, "ctx", 2)
    state_far, kv_far, code_far = from_far

    link_2 = (code_far[-1] == code_2[0]) & (code_2[0] == code_1[-1])
    carry_scale = jnp.where(link_2, decay_2 * decay_1, 0.0)
    incoming_state = pair_state + carry_scale[:, None, None] * state_far.astype(F32)

    query_heads = light_query.reshape(tok_rows, heads_here, head_size)
    carried_in = jnp.einsum(
        "thd,hde->the", query_heads.astype(F32), incoming_state, precision=lax.Precision.HIGHEST
    )
    uses_state = code == code_1[-1]
    scale_in = jnp.where(uses_state[None, :], jnp.exp(decay_sum), 0.0)
    mixed = mixed + carried_in * scale_in.T[:, :, None]
    squares = jnp.sum(mixed * mixed, axis=(1, 2))
    squares = lax.psum(squares, "tensor")
    features = heads_here * head_size * lax.axis_size("tensor")
    inverse = lax.rsqrt(squares / features + 1e-06)
    gate_open = jax.nn.sigmoid(light_gate.astype(F32)).reshape(tok_rows, heads_here, head_size)
    normed = mixed * inverse[:, None, None] * norm_gain.reshape(heads_here, head_size) * gate_open
    light_out = normed.reshape(tok_rows, heads_here * head_size).astype(BF16)

    kv_window = jnp.concatenate([kv_far[0], kv_far[1], kv_2, kv_1, soft_kv], axis=0)
    code_window = jnp.concatenate([code_far, code_2, code_1, code])
    soft_out = soft_window(
        soft_query, kv_window[:, :kv_cols], kv_window[:, kv_cols:], code, code_window, heads_here
    )
    return (light_out, soft_out)


def solution(mesh):
    in_specs = (
        P(("groups", "ctx"), "tensor"),
        P(("groups", "ctx"), "tensor"),
        P(("groups", "ctx"), "tensor"),
        P(("groups", "ctx"), "tensor"),
        P("tensor", ("groups", "ctx")),
        P("tensor"),
        P(("groups", "ctx"), "tensor"),
        P(("groups", "ctx"), "tensor"),
        P(("groups", "ctx"), "tensor"),
        P(("groups", "ctx")),
    )
    out_specs = (P(("groups", "ctx"), "tensor"), P(("groups", "ctx"), "tensor"))
    return jax.shard_map(
        on_device, mesh=mesh, in_specs=in_specs, out_specs=out_specs, check_vma=False
    )
```

```python
import jax
import jax.numpy as jnp
from jax import lax
from jax.sharding import PartitionSpec as P

NEG_BIG = -1e30
MAXDOC = 512
F32 = jnp.float32
BF16 = jnp.bfloat16


def shifted(block, axis, distance):
    devices = lax.axis_size(axis)
    route = [(i, i + distance) for i in range(devices - distance)]
    return lax.ppermute(block, axis, route)


def light_local(light_query, light_key, light_value, decay_sum, code):
    tok_rows, heads_here = light_query.shape[0], decay_sum.shape[0]
    head_size = light_query.shape[1] // heads_here
    query_heads = light_query.reshape(tok_rows, heads_here, head_size)
    key_heads = light_key.reshape(tok_rows, heads_here, head_size)
    value_heads = light_value.reshape(tok_rows, heads_here, head_size)
    token_position = jnp.arange(tok_rows)
    allowed = (code[:, None] == code[None, :]) & (token_position[None, :] <= token_position[:, None])
    decay_gap = jnp.where(allowed[None], decay_sum[:, :, None] - decay_sum[:, None, :], -jnp.inf)
    products = jnp.einsum("thd,shd->hts", query_heads, key_heads, preferred_element_type=F32)
    weights = (products * jnp.exp(decay_gap)).astype(BF16)
    mixed = jnp.einsum("hts,shd->thd", weights, value_heads, preferred_element_type=F32)
    to_end = jnp.where((code == code[-1])[None, :], jnp.exp(decay_sum[:, -1:] - decay_sum), 0.0)
    key_weighted = (key_heads * to_end.T[:, :, None]).astype(BF16)
    local_state = jnp.einsum("shd,she->hde", key_weighted, value_heads, preferred_element_type=F32)
    return mixed, local_state


def soft_window(soft_query, key_heads, value_heads, code, code_window, heads_here):
    tok_rows = soft_query.shape[0]
    kv_here, span, head_size = key_heads.shape
    group = heads_here // kv_here
    queries = soft_query.reshape(tok_rows, kv_here, group, head_size)
    key_position = jnp.arange(span)
    query_position = jnp.arange(tok_rows) + (span - tok_rows)
    allowed = (code[:, None] == code_window[None, :]) & (key_position[None, :] <= query_position[:, None])
    scores = jnp.einsum("tkgd,ksd->kgts", queries, key_heads, preferred_element_type=F32) * head_size ** (-0.5)
    scores = jnp.where(allowed, scores, NEG_BIG)
    row_max = jnp.max(scores, axis=-1)
    prob_block = jnp.exp(scores - row_max[..., None])
    row_total = jnp.sum(prob_block, axis=-1)
    weighted = jnp.einsum("kgts,ksd->kgtd", prob_block.astype(BF16), value_heads, preferred_element_type=F32)
    output = (weighted / row_total[..., None]).transpose(2, 0, 1, 3).reshape(tok_rows, heads_here * head_size)
    return output.astype(BF16)


def split_parts(value):
    high = lax.reduce_precision(value, exponent_bits=8, mantissa_bits=7)
    rest = value - high
    middle = lax.reduce_precision(rest, exponent_bits=8, mantissa_bits=7)
    return jnp.concatenate([high, middle, rest - middle])


def join_parts(parts):
    third = parts.shape[0] // 3
    parts = parts.astype(F32)
    return (parts[:third] + parts[third : 2 * third]) + parts[2 * third :]


def rows_of(flat, width):
    tile = 16 * width
    padded = -(-flat.shape[0] // tile) * tile
    return jnp.pad(flat, (0, padded - flat.shape[0])).reshape(-1, width).astype(BF16)


def on_device(
    light_query,
    light_key,
    light_value,
    light_gate,
    log_decay,
    norm_gain,
    soft_query,
    soft_key,
    soft_value,
    segment_ids,
):
    tok_rows = light_query.shape[0]
    heads_here = log_decay.shape[0]
    head_size = light_query.shape[1] // heads_here
    kv_here = soft_key.shape[1] // head_size
    assert -(-MAXDOC // tok_rows) == 4
    code = segment_ids.astype(F32) + 1.0
    decay_sum = jnp.cumsum(log_decay, axis=1)

    mixed, local_state = light_local(light_query, light_key, light_value, decay_sum, code)
    block_decay = jnp.exp(decay_sum[:, -1])

    own_keys = soft_key.reshape(tok_rows, kv_here, head_size).transpose(1, 0, 2)
    own_values = soft_value.reshape(tok_rows, kv_here, head_size).transpose(1, 0, 2)
    state_rows = heads_here * head_size
    kv_rows = kv_here * tok_rows
    own = jnp.concatenate(
        [
            local_state.astype(BF16).reshape(state_rows, head_size),
            own_keys.reshape(kv_rows, head_size),
            own_values.reshape(kv_rows, head_size),
            rows_of(jnp.concatenate([code, split_parts(block_decay)]), head_size),
        ]
    )
    from_1 = shifted(own, "ctx", 1)
    from_2 = shifted(own, "ctx", 2)

    def unpack(block):
        state = block[:state_rows].reshape(heads_here, head_size, head_size).astype(F32)
        keys = block[state_rows : state_rows + kv_rows].reshape(kv_here, tok_rows, head_size)
        values = block[state_rows + kv_rows : state_rows + 2 * kv_rows].reshape(kv_here, tok_rows, head_size)
        meta = block[state_rows + 2 * kv_rows :].reshape(-1)
        codes = meta[:tok_rows].astype(F32)
        decay = join_parts(meta[tok_rows : tok_rows + 3 * heads_here])
        return state, keys, values, codes, decay

    state_1, keys_1, values_1, code_1, decay_1 = unpack(from_1)
    state_2, keys_2, values_2, code_2, decay_2 = unpack(from_2)

    link_1 = (code_2[-1] == code_1[0]) & (code_1[0] == code_1[-1])
    pair_state = state_1 + jnp.where(link_1, decay_1, 0.0)[:, None, None] * state_2

    relay = jnp.concatenate(
        [
            pair_state.astype(BF16).reshape(state_rows, head_size),
            keys_2.reshape(kv_rows, head_size),
            keys_1.reshape(kv_rows, head_size),
            values_2.reshape(kv_rows, head_size),
            values_1.reshape(kv_rows, head_size),
            rows_of(jnp.concatenate([code_2, code_1]), head_size),
        ]
    )
    from_far = shifted(relay, "ctx", 2)
    state_far = from_far[:state_rows].reshape(heads_here, head_size, head_size).astype(F32)
    keys_far = from_far[state_rows : state_rows + 2 * kv_rows].reshape(2, kv_here, tok_rows, head_size)
    values_far = from_far[state_rows + 2 * kv_rows : state_rows + 4 * kv_rows].reshape(
        2, kv_here, tok_rows, head_size
    )
    code_far = from_far[state_rows + 4 * kv_rows :].reshape(-1)[: 2 * tok_rows].astype(F32)

    link_2 = (code_far[-1] == code_2[0]) & (code_2[0] == code_1[-1])
    carry_scale = jnp.where(link_2, decay_2 * decay_1, 0.0)
    incoming_state = pair_state + carry_scale[:, None, None] * state_far

    query_heads = light_query.reshape(tok_rows, heads_here, head_size)
    carried_in = jnp.einsum(
        "thd,hde->the", query_heads.astype(F32), incoming_state, precision=lax.Precision.HIGHEST
    )
    uses_state = code == code_1[-1]
    scale_in = jnp.where(uses_state[None, :], jnp.exp(decay_sum), 0.0)
    mixed = mixed + carried_in * scale_in.T[:, :, None]
    squares = jnp.sum(mixed * mixed, axis=(1, 2))
    squares = lax.psum(squares, "tensor")
    features = heads_here * head_size * lax.axis_size("tensor")
    inverse = lax.rsqrt(squares / features + 1e-06)
    gate_open = jax.nn.sigmoid(light_gate.astype(F32)).reshape(tok_rows, heads_here, head_size)
    normed = mixed * inverse[:, None, None] * norm_gain.reshape(heads_here, head_size) * gate_open
    light_out = normed.reshape(tok_rows, heads_here * head_size).astype(BF16)

    key_window = jnp.concatenate([keys_far[0], keys_far[1], keys_2, keys_1, own_keys], axis=1)
    value_window = jnp.concatenate([values_far[0], values_far[1], values_2, values_1, own_values], axis=1)
    code_window = jnp.concatenate([code_far, code_2, code_1, code])
    soft_out = soft_window(soft_query, key_window, value_window, code, code_window, heads_here)
    return (light_out, soft_out)


def solution(mesh):
    in_specs = (
        P(("groups", "ctx"), "tensor"),
        P(("groups", "ctx"), "tensor"),
        P(("groups", "ctx"), "tensor"),
        P(("groups", "ctx"), "tensor"),
        P("tensor", ("groups", "ctx")),
        P("tensor"),
        P(("groups", "ctx"), "tensor"),
        P(("groups", "ctx"), "tensor"),
        P(("groups", "ctx"), "tensor"),
        P(("groups", "ctx")),
    )
    out_specs = (P(("groups", "ctx"), "tensor"), P(("groups", "ctx"), "tensor"))
    return jax.shard_map(
        on_device, mesh=mesh, in_specs=in_specs, out_specs=out_specs, check_vma=False
    )
```

```python
import jax
import jax.numpy as jnp
from jax import lax
from jax.sharding import PartitionSpec as P

NEG_BIG = -1e30
MAXDOC = 512
F32 = jnp.float32
BF16 = jnp.bfloat16


def shifted(block, axis, distance):
    devices = lax.axis_size(axis)
    route = [(i, i + distance) for i in range(devices - distance)]
    return lax.ppermute(block, axis, route)


def light_local(light_query, light_key, light_value, decay_sum, code):
    tok_rows, heads_here = light_query.shape[0], decay_sum.shape[0]
    head_size = light_query.shape[1] // heads_here
    query_heads = light_query.reshape(tok_rows, heads_here, head_size)
    key_heads = light_key.reshape(tok_rows, heads_here, head_size)
    value_heads = light_value.reshape(tok_rows, heads_here, head_size)
    token_position = jnp.arange(tok_rows)
    allowed = (code[:, None] == code[None, :]) & (token_position[None, :] <= token_position[:, None])
    decay_gap = jnp.where(allowed[None], decay_sum[:, :, None] - decay_sum[:, None, :], -jnp.inf)
    products = jnp.einsum("thd,shd->hts", query_heads, key_heads, preferred_element_type=F32)
    weights = (products * jnp.exp(decay_gap)).astype(BF16)
    mixed = jnp.einsum("hts,shd->thd", weights, value_heads, preferred_element_type=F32)
    to_end = jnp.where((code == code[-1])[None, :], jnp.exp(decay_sum[:, -1:] - decay_sum), 0.0)
    key_weighted = (key_heads * to_end.T[:, :, None]).astype(BF16)
    local_state = jnp.einsum("shd,she->hde", key_weighted, value_heads, preferred_element_type=F32)
    return mixed, local_state


def soft_window(soft_query, key_heads, value_heads, code, code_window, heads_here):
    tok_rows = soft_query.shape[0]
    kv_here, span, head_size = key_heads.shape
    group = heads_here // kv_here
    queries = soft_query.reshape(tok_rows, kv_here, group, head_size)
    key_position = jnp.arange(span)
    query_position = jnp.arange(tok_rows) + (span - tok_rows)
    allowed = (code[:, None] == code_window[None, :]) & (key_position[None, :] <= query_position[:, None])
    scores = jnp.einsum("tkgd,ksd->kgts", queries, key_heads, preferred_element_type=F32) * head_size ** (-0.5)
    scores = jnp.where(allowed, scores, NEG_BIG)
    row_max = jnp.max(scores, axis=-1)
    prob_block = jnp.exp(scores - row_max[..., None])
    row_total = jnp.sum(prob_block, axis=-1)
    weighted = jnp.einsum("kgts,ksd->kgtd", prob_block.astype(BF16), value_heads, preferred_element_type=F32)
    output = (weighted / row_total[..., None]).transpose(2, 0, 1, 3).reshape(tok_rows, heads_here * head_size)
    return output.astype(BF16)


def split_parts(value):
    high = lax.reduce_precision(value, exponent_bits=8, mantissa_bits=7)
    rest = value - high
    middle = lax.reduce_precision(rest, exponent_bits=8, mantissa_bits=7)
    return jnp.concatenate([high, middle, rest - middle])


def join_parts(parts):
    third = parts.shape[0] // 3
    parts = parts.astype(F32)
    return (parts[:third] + parts[third : 2 * third]) + parts[2 * third :]


def rows_of(flat, width):
    tile = 16 * width
    padded = -(-flat.shape[0] // tile) * tile
    return jnp.pad(flat, (0, padded - flat.shape[0])).reshape(-1, width).astype(BF16)


def on_device(
    light_query,
    light_key,
    light_value,
    light_gate,
    log_decay,
    norm_gain,
    soft_query,
    soft_key,
    soft_value,
    segment_ids,
):
    tok_rows = light_query.shape[0]
    heads_here = log_decay.shape[0]
    head_size = light_query.shape[1] // heads_here
    kv_here = soft_key.shape[1] // head_size
    assert -(-MAXDOC // tok_rows) == 4
    code = segment_ids.astype(F32) + 1.0
    decay_sum = jnp.cumsum(log_decay, axis=1)

    mixed, local_state = light_local(light_query, light_key, light_value, decay_sum, code)
    block_decay = jnp.exp(decay_sum[:, -1])

    own_keys = soft_key.reshape(tok_rows, kv_here, head_size).transpose(1, 0, 2)
    own_values = soft_value.reshape(tok_rows, kv_here, head_size).transpose(1, 0, 2)
    state_rows = heads_here * head_size
    kv_rows = kv_here * tok_rows
    own = jnp.concatenate(
        [
            local_state.astype(BF16).reshape(state_rows, head_size),
            own_keys.reshape(kv_rows, head_size),
            own_values.reshape(kv_rows, head_size),
            rows_of(jnp.concatenate([code, split_parts(block_decay)]), head_size),
        ]
    )
    from_1 = shifted(own, "ctx", 1)
    from_2 = shifted(own, "ctx", 2)
    kv_only = jnp.concatenate(
        [
            own_keys.reshape(kv_rows, head_size),
            own_values.reshape(kv_rows, head_size),
            rows_of(code, head_size),
        ]
    )
    from_3 = shifted(kv_only, "ctx", 3)
    from_4 = shifted(kv_only, "ctx", 4)

    def unpack(block):
        state = block[:state_rows].reshape(heads_here, head_size, head_size).astype(F32)
        keys = block[state_rows : state_rows + kv_rows].reshape(kv_here, tok_rows, head_size)
        values = block[state_rows + kv_rows : state_rows + 2 * kv_rows].reshape(kv_here, tok_rows, head_size)
        meta = block[state_rows + 2 * kv_rows :].reshape(-1)
        codes = meta[:tok_rows].astype(F32)
        decay = join_parts(meta[tok_rows : tok_rows + 3 * heads_here])
        return state, keys, values, codes, decay

    def unpack_kv(block):
        keys = block[:kv_rows].reshape(kv_here, tok_rows, head_size)
        values = block[kv_rows : 2 * kv_rows].reshape(kv_here, tok_rows, head_size)
        codes = block[2 * kv_rows :].reshape(-1)[:tok_rows].astype(F32)
        return keys, values, codes

    state_1, keys_1, values_1, code_1, decay_1 = unpack(from_1)
    state_2, keys_2, values_2, code_2, decay_2 = unpack(from_2)
    keys_3, values_3, code_3 = unpack_kv(from_3)
    keys_4, values_4, code_4 = unpack_kv(from_4)

    link_1 = (code_2[-1] == code_1[0]) & (code_1[0] == code_1[-1])
    pair_state = state_1 + jnp.where(link_1, decay_1, 0.0)[:, None, None] * state_2

    from_far = shifted(pair_state.astype(BF16), "ctx", 2)
    state_far = from_far.astype(F32)

    link_2 = (code_3[-1] == code_2[0]) & (code_2[0] == code_1[-1])
    carry_scale = jnp.where(link_2, decay_2 * decay_1, 0.0)
    incoming_state = pair_state + carry_scale[:, None, None] * state_far

    query_heads = light_query.reshape(tok_rows, heads_here, head_size)
    carried_in = jnp.einsum(
        "thd,hde->the", query_heads.astype(F32), incoming_state, precision=lax.Precision.HIGHEST
    )
    uses_state = code == code_1[-1]
    scale_in = jnp.where(uses_state[None, :], jnp.exp(decay_sum), 0.0)
    mixed = mixed + carried_in * scale_in.T[:, :, None]
    squares = jnp.sum(mixed * mixed, axis=(1, 2))
    squares = lax.psum(squares, "tensor")
    features = heads_here * head_size * lax.axis_size("tensor")
    inverse = lax.rsqrt(squares / features + 1e-06)
    gate_open = jax.nn.sigmoid(light_gate.astype(F32)).reshape(tok_rows, heads_here, head_size)
    normed = mixed * inverse[:, None, None] * norm_gain.reshape(heads_here, head_size) * gate_open
    light_out = normed.reshape(tok_rows, heads_here * head_size).astype(BF16)

    key_window = jnp.concatenate([keys_4, keys_3, keys_2, keys_1, own_keys], axis=1)
    value_window = jnp.concatenate([values_4, values_3, values_2, values_1, own_values], axis=1)
    code_window = jnp.concatenate([code_4, code_3, code_2, code_1, code])
    soft_out = soft_window(soft_query, key_window, value_window, code, code_window, heads_here)
    return (light_out, soft_out)


def solution(mesh):
    in_specs = (
        P(("groups", "ctx"), "tensor"),
        P(("groups", "ctx"), "tensor"),
        P(("groups", "ctx"), "tensor"),
        P(("groups", "ctx"), "tensor"),
        P("tensor", ("groups", "ctx")),
        P("tensor"),
        P(("groups", "ctx"), "tensor"),
        P(("groups", "ctx"), "tensor"),
        P(("groups", "ctx"), "tensor"),
        P(("groups", "ctx")),
    )
    out_specs = (P(("groups", "ctx"), "tensor"), P(("groups", "ctx"), "tensor"))
    return jax.shard_map(
        on_device, mesh=mesh, in_specs=in_specs, out_specs=out_specs, check_vma=False
    )
```

```python
import jax
import jax.numpy as jnp
from jax import lax
from jax.sharding import PartitionSpec as P


NEG_BIG = -1e30
MAXDOC = 512
F32 = jnp.float32
BF16 = jnp.bfloat16


def shifted(block, axis, distance):
    devices = lax.axis_size(axis)
    route = [(i, i + distance) for i in range(devices - distance)]
    return lax.ppermute(block, axis, route)


def light_local(light_query, light_key, light_value, decay_sum, code):
    tok_rows, heads_here = light_query.shape[0], decay_sum.shape[0]
    head_size = light_query.shape[1] // heads_here
    query_heads = light_query.reshape(tok_rows, heads_here, head_size)
    key_heads = light_key.reshape(tok_rows, heads_here, head_size)
    value_heads = light_value.reshape(tok_rows, heads_here, head_size)
    token_position = jnp.arange(tok_rows)
    allowed = (code[:, None] == code[None, :]) & (token_position[None, :] <= token_position[:, None])
    decay_gap = jnp.where(allowed[None], decay_sum[:, :, None] - decay_sum[:, None, :], -jnp.inf)
    products = jnp.einsum("thd,shd->hts", query_heads, key_heads, preferred_element_type=F32)
    weights = (products * jnp.exp(decay_gap)).astype(BF16)
    mixed = jnp.einsum("hts,shd->thd", weights, value_heads, preferred_element_type=F32)
    to_end = jnp.where((code == code[-1])[None, :], jnp.exp(decay_sum[:, -1:] - decay_sum), 0.0)
    key_weighted = (key_heads * to_end.T[:, :, None]).astype(BF16)
    local_state = jnp.einsum("shd,she->hde", key_weighted, value_heads, preferred_element_type=F32)
    return mixed, local_state


def soft_window(soft_query, key_heads, value_heads, code, code_window, heads_here):
    tok_rows = soft_query.shape[0]
    kv_here, span, head_size = key_heads.shape
    group = heads_here // kv_here
    queries = soft_query.reshape(tok_rows, kv_here, group, head_size)
    key_position = jnp.arange(span)
    query_position = jnp.arange(tok_rows) + (span - tok_rows)
    allowed = (code[:, None] == code_window[None, :]) & (key_position[None, :] <= query_position[:, None])
    scores = jnp.einsum("tkgd,ksd->kgts", queries, key_heads, preferred_element_type=F32) * head_size ** (-0.5)
    scores = jnp.where(allowed, scores, NEG_BIG)
    row_max = jnp.max(scores, axis=-1)
    prob_block = jnp.exp(scores - row_max[..., None])
    row_total = jnp.sum(prob_block, axis=-1)
    weighted = jnp.einsum("kgts,ksd->kgtd", prob_block.astype(BF16), value_heads, preferred_element_type=F32)
    output = (weighted / row_total[..., None]).transpose(2, 0, 1, 3).reshape(tok_rows, heads_here * head_size)
    return output.astype(BF16)


def split_parts(value):
    high = lax.reduce_precision(value, exponent_bits=8, mantissa_bits=7)
    rest = value - high
    middle = lax.reduce_precision(rest, exponent_bits=8, mantissa_bits=7)
    return jnp.concatenate([high, middle, rest - middle])


def join_parts(parts):
    third = parts.shape[0] // 3
    parts = parts.astype(F32)
    return (parts[:third] + parts[third : 2 * third]) + parts[2 * third :]


def rows_of(flat, width):
    tile = 16 * width
    padded = -(-flat.shape[0] // tile) * tile
    return jnp.pad(flat, (0, padded - flat.shape[0])).reshape(-1, width).astype(BF16)


def on_device_body(
    light_query,
    light_key,
    light_value,
    light_gate,
    log_decay,
    norm_gain,
    soft_query,
    soft_key,
    soft_value,
    segment_ids,
):
    tok_rows = light_query.shape[0]
    heads_here = log_decay.shape[0]
    head_size = light_query.shape[1] // heads_here
    kv_here = soft_key.shape[1] // head_size
    assert -(-MAXDOC // tok_rows) == 4
    code = segment_ids.astype(F32) + 1.0
    decay_sum = jnp.cumsum(log_decay, axis=1)

    mixed, local_state = light_local(light_query, light_key, light_value, decay_sum, code)
    block_decay = jnp.exp(decay_sum[:, -1])

    own_keys = soft_key.reshape(tok_rows, kv_here, head_size).transpose(1, 0, 2)
    own_values = soft_value.reshape(tok_rows, kv_here, head_size).transpose(1, 0, 2)
    state_rows = heads_here * head_size
    kv_rows = kv_here * tok_rows
    own = jnp.concatenate(
        [
            local_state.astype(BF16).reshape(state_rows, head_size),
            own_keys.reshape(kv_rows, head_size),
            own_values.reshape(kv_rows, head_size),
            rows_of(jnp.concatenate([code, split_parts(block_decay)]), head_size),
        ]
    )
    from_1 = shifted(own, "ctx", 1)
    from_2 = shifted(own, "ctx", 2)
    kv_only = jnp.concatenate(
        [
            own_keys.reshape(kv_rows, head_size),
            own_values.reshape(kv_rows, head_size),
            rows_of(code, head_size),
        ]
    )
    from_3 = shifted(kv_only, "ctx", 3)
    from_4 = shifted(kv_only, "ctx", 4)

    def unpack(block):
        state = block[:state_rows].reshape(heads_here, head_size, head_size).astype(F32)
        keys = block[state_rows : state_rows + kv_rows].reshape(kv_here, tok_rows, head_size)
        values = block[state_rows + kv_rows : state_rows + 2 * kv_rows].reshape(kv_here, tok_rows, head_size)
        meta = block[state_rows + 2 * kv_rows :].reshape(-1)
        codes = meta[:tok_rows].astype(F32)
        decay = join_parts(meta[tok_rows : tok_rows + 3 * heads_here])
        return state, keys, values, codes, decay

    def unpack_kv(block):
        keys = block[:kv_rows].reshape(kv_here, tok_rows, head_size)
        values = block[kv_rows : 2 * kv_rows].reshape(kv_here, tok_rows, head_size)
        codes = block[2 * kv_rows :].reshape(-1)[:tok_rows].astype(F32)
        return keys, values, codes

    state_1, keys_1, values_1, code_1, decay_1 = unpack(from_1)
    state_2, keys_2, values_2, code_2, decay_2 = unpack(from_2)
    keys_3, values_3, code_3 = unpack_kv(from_3)
    keys_4, values_4, code_4 = unpack_kv(from_4)

    link_1 = (code_2[-1] == code_1[0]) & (code_1[0] == code_1[-1])
    pair_state = state_1 + jnp.where(link_1, decay_1, 0.0)[:, None, None] * state_2

    from_far = shifted(pair_state.astype(BF16), "ctx", 2)
    state_far = from_far.astype(F32)

    link_2 = (code_3[-1] == code_2[0]) & (code_2[0] == code_1[-1])
    carry_scale = jnp.where(link_2, decay_2 * decay_1, 0.0)
    incoming_state = pair_state + carry_scale[:, None, None] * state_far

    query_heads = light_query.reshape(tok_rows, heads_here, head_size)
    carried_in = jnp.einsum(
        "thd,hde->the", query_heads.astype(F32), incoming_state, precision=lax.Precision.HIGHEST
    )
    uses_state = code == code_1[-1]
    scale_in = jnp.where(uses_state[None, :], jnp.exp(decay_sum), 0.0)
    mixed = mixed + carried_in * scale_in.T[:, :, None]
    squares = jnp.sum(mixed * mixed, axis=(1, 2))
    squares = lax.psum(squares, "tensor")
    features = heads_here * head_size * lax.axis_size("tensor")
    inverse = lax.rsqrt(squares / features + 1e-06)
    gate_open = jax.nn.sigmoid(light_gate.astype(F32)).reshape(tok_rows, heads_here, head_size)
    normed = mixed * inverse[:, None, None] * norm_gain.reshape(heads_here, head_size) * gate_open
    light_out = normed.reshape(tok_rows, heads_here * head_size).astype(BF16)

    key_window = jnp.concatenate([keys_4, keys_3, keys_2, keys_1, own_keys], axis=1)
    value_window = jnp.concatenate([values_4, values_3, values_2, values_1, own_values], axis=1)
    code_window = jnp.concatenate([code_4, code_3, code_2, code_1, code])
    soft_out = soft_window(soft_query, key_window, value_window, code, code_window, heads_here)
    return (light_out, soft_out)


def solution(mesh):
    in_specs = (
        P(("groups", "ctx"), "tensor"),
        P(("groups", "ctx"), "tensor"),
        P(("groups", "ctx"), "tensor"),
        P(("groups", "ctx"), "tensor"),
        P("tensor", ("groups", "ctx")),
        P("tensor"),
        P(("groups", "ctx"), "tensor"),
        P(("groups", "ctx"), "tensor"),
        P(("groups", "ctx"), "tensor"),
        P(("groups", "ctx")),
    )
    out_specs = (P(("groups", "ctx"), "tensor"), P(("groups", "ctx"), "tensor"))
    return jax.shard_map(on_device_body, mesh=mesh, in_specs=in_specs, out_specs=out_specs, check_vma=False)
```

```python
import jax
import jax.numpy as jnp
from jax import lax
from jax.sharding import PartitionSpec as P


NEG_BIG = -1e30
MAXDOC = 512
F32 = jnp.float32
BF16 = jnp.bfloat16


def shifted(block, axis, distance):
    devices = lax.axis_size(axis)
    route = [(i, i + distance) for i in range(devices - distance)]
    return lax.ppermute(block, axis, route)


def light_local(light_query, light_key, light_value, decay_sum, code):
    tok_rows, heads_here = light_query.shape[0], decay_sum.shape[0]
    head_size = light_query.shape[1] // heads_here
    query_heads = light_query.reshape(tok_rows, heads_here, head_size)
    key_heads = light_key.reshape(tok_rows, heads_here, head_size)
    value_heads = light_value.reshape(tok_rows, heads_here, head_size)
    token_position = jnp.arange(tok_rows)
    allowed = (code[:, None] == code[None, :]) & (token_position[None, :] <= token_position[:, None])
    decay_gap = jnp.where(allowed[None], decay_sum[:, :, None] - decay_sum[:, None, :], -jnp.inf)
    products = jnp.einsum("thd,shd->hts", query_heads, key_heads, preferred_element_type=F32)
    weights = (products * jnp.exp(decay_gap)).astype(BF16)
    mixed = jnp.einsum("hts,shd->thd", weights, value_heads, preferred_element_type=F32)
    to_end = jnp.where((code == code[-1])[None, :], jnp.exp(decay_sum[:, -1:] - decay_sum), 0.0)
    key_weighted = (key_heads * to_end.T[:, :, None]).astype(BF16)
    local_state = jnp.einsum("shd,she->hde", key_weighted, value_heads, preferred_element_type=F32)
    return mixed, local_state


def soft_window(soft_query, key_heads, value_heads, code, code_window, heads_here):
    tok_rows = soft_query.shape[0]
    kv_here, span, head_size = key_heads.shape
    group = heads_here // kv_here
    queries = soft_query.reshape(tok_rows, kv_here, group, head_size)
    key_position = jnp.arange(span)
    query_position = jnp.arange(tok_rows) + (span - tok_rows)
    allowed = (code[:, None] == code_window[None, :]) & (key_position[None, :] <= query_position[:, None])
    scores = jnp.einsum("tkgd,ksd->kgts", queries, key_heads, preferred_element_type=F32) * head_size ** (-0.5)
    scores = jnp.where(allowed, scores, NEG_BIG)
    row_max = jnp.max(scores, axis=-1)
    prob_block = jnp.exp(scores - row_max[..., None])
    row_total = jnp.sum(prob_block, axis=-1)
    weighted = jnp.einsum("kgts,ksd->kgtd", prob_block.astype(BF16), value_heads, preferred_element_type=F32)
    output = (weighted / row_total[..., None]).transpose(2, 0, 1, 3).reshape(tok_rows, heads_here * head_size)
    return output.astype(BF16)


def split_parts(value):
    high = lax.reduce_precision(value, exponent_bits=8, mantissa_bits=7)
    rest = value - high
    middle = lax.reduce_precision(rest, exponent_bits=8, mantissa_bits=7)
    return jnp.concatenate([high, middle, rest - middle])


def join_parts(parts):
    third = parts.shape[0] // 3
    parts = parts.astype(F32)
    return (parts[:third] + parts[third : 2 * third]) + parts[2 * third :]


def rows_of(flat, width):
    tile = 16 * width
    padded = -(-flat.shape[0] // tile) * tile
    return jnp.pad(flat, (0, padded - flat.shape[0])).reshape(-1, width).astype(BF16)


def on_device_body(
    light_query,
    light_key,
    light_value,
    light_gate,
    log_decay,
    norm_gain,
    soft_query,
    soft_key,
    soft_value,
    segment_ids,
):
    tok_rows = light_query.shape[0]
    heads_here = log_decay.shape[0]
    head_size = light_query.shape[1] // heads_here
    kv_here = soft_key.shape[1] // head_size
    assert -(-MAXDOC // tok_rows) == 4
    code = segment_ids.astype(F32) + 1.0
    decay_sum = jnp.cumsum(log_decay, axis=1)

    mixed, local_state = light_local(light_query, light_key, light_value, decay_sum, code)
    block_decay = jnp.exp(decay_sum[:, -1])

    own_keys = soft_key.reshape(tok_rows, kv_here, head_size).transpose(1, 0, 2)
    own_values = soft_value.reshape(tok_rows, kv_here, head_size).transpose(1, 0, 2)
    state_rows = heads_here * head_size
    kv_rows = kv_here * tok_rows
    own = jnp.concatenate(
        [
            local_state.astype(BF16).reshape(state_rows, head_size),
            own_keys.reshape(kv_rows, head_size),
            own_values.reshape(kv_rows, head_size),
            rows_of(jnp.concatenate([code, split_parts(block_decay)]), head_size),
        ]
    )
    from_1 = shifted(own, "ctx", 1)
    from_2 = shifted(own, "ctx", 2)
    kv_only = jnp.concatenate(
        [
            own_keys.reshape(kv_rows, head_size),
            own_values.reshape(kv_rows, head_size),
            rows_of(code, head_size),
        ]
    )
    from_3 = shifted(kv_only, "ctx", 3)
    from_4 = shifted(kv_only, "ctx", 4)

    def unpack(block):
        state = block[:state_rows].reshape(heads_here, head_size, head_size).astype(F32)
        meta = block[state_rows + 2 * kv_rows :].reshape(-1)
        codes = meta[:tok_rows].astype(F32)
        decay = join_parts(meta[tok_rows : tok_rows + 3 * heads_here])
        return state, codes, decay

    def unpack_near_kv(block):
        keys = block[state_rows : state_rows + kv_rows].reshape(kv_here, tok_rows, head_size)
        values = block[state_rows + kv_rows : state_rows + 2 * kv_rows].reshape(kv_here, tok_rows, head_size)
        return keys, values

    def unpack_kv(block):
        keys = block[:kv_rows].reshape(kv_here, tok_rows, head_size)
        values = block[kv_rows : 2 * kv_rows].reshape(kv_here, tok_rows, head_size)
        codes = block[2 * kv_rows :].reshape(-1)[:tok_rows].astype(F32)
        return keys, values, codes

    state_1, code_1, decay_1 = unpack(from_1)
    state_2, code_2, decay_2 = unpack(from_2)
    code_3 = from_3[2 * kv_rows :].reshape(-1)[:tok_rows].astype(F32)

    link_1 = (code_2[-1] == code_1[0]) & (code_1[0] == code_1[-1])
    pair_state = state_1 + jnp.where(link_1, decay_1, 0.0)[:, None, None] * state_2

    from_far = shifted(pair_state.astype(BF16), "ctx", 2)
    state_far = from_far.astype(F32)

    link_2 = (code_3[-1] == code_2[0]) & (code_2[0] == code_1[-1])
    carry_scale = jnp.where(link_2, decay_2 * decay_1, 0.0)
    incoming_state = pair_state + carry_scale[:, None, None] * state_far

    query_heads = light_query.reshape(tok_rows, heads_here, head_size)
    carried_in = jnp.einsum(
        "thd,hde->the", query_heads.astype(F32), incoming_state, precision=lax.Precision.HIGHEST
    )
    uses_state = code == code_1[-1]
    scale_in = jnp.where(uses_state[None, :], jnp.exp(decay_sum), 0.0)
    mixed = mixed + carried_in * scale_in.T[:, :, None]
    squares = jnp.sum(mixed * mixed, axis=(1, 2))
    squares = lax.psum(squares, "tensor")
    features = heads_here * head_size * lax.axis_size("tensor")
    inverse = lax.rsqrt(squares / features + 1e-06)
    gate_open = jax.nn.sigmoid(light_gate.astype(F32)).reshape(tok_rows, heads_here, head_size)
    normed = mixed * inverse[:, None, None] * norm_gain.reshape(heads_here, head_size) * gate_open
    light_out = normed.reshape(tok_rows, heads_here * head_size).astype(BF16)

    keys_1, values_1 = unpack_near_kv(from_1)
    keys_2, values_2 = unpack_near_kv(from_2)
    keys_3, values_3, code_3 = unpack_kv(from_3)
    keys_4, values_4, code_4 = unpack_kv(from_4)
    key_window = jnp.concatenate([keys_4, keys_3, keys_2, keys_1, own_keys], axis=1)
    value_window = jnp.concatenate([values_4, values_3, values_2, values_1, own_values], axis=1)
    code_window = jnp.concatenate([code_4, code_3, code_2, code_1, code])
    soft_out = soft_window(soft_query, key_window, value_window, code, code_window, heads_here)
    return (light_out, soft_out)


def solution(mesh):
    in_specs = (
        P(("groups", "ctx"), "tensor"),
        P(("groups", "ctx"), "tensor"),
        P(("groups", "ctx"), "tensor"),
        P(("groups", "ctx"), "tensor"),
        P("tensor", ("groups", "ctx")),
        P("tensor"),
        P(("groups", "ctx"), "tensor"),
        P(("groups", "ctx"), "tensor"),
        P(("groups", "ctx"), "tensor"),
        P(("groups", "ctx")),
    )
    out_specs = (P(("groups", "ctx"), "tensor"), P(("groups", "ctx"), "tensor"))
    return jax.shard_map(on_device_body, mesh=mesh, in_specs=in_specs, out_specs=out_specs, check_vma=False)
```

```python
import jax
import jax.numpy as jnp
from jax import lax
from jax.sharding import PartitionSpec as P

NEG_BIG = -1e30
MAXDOC = 512
F32 = jnp.float32
BF16 = jnp.bfloat16


def shifted(block, axis, distance):
    devices = lax.axis_size(axis)
    route = [(i, i + distance) for i in range(devices - distance)]
    return lax.ppermute(block, axis, route)


def light_local(light_query, light_key, light_value, decay_sum, code):
    tok_rows, heads_here = light_query.shape[0], decay_sum.shape[0]
    head_size = light_query.shape[1] // heads_here
    query_heads = light_query.reshape(tok_rows, heads_here, head_size)
    key_heads = light_key.reshape(tok_rows, heads_here, head_size)
    value_heads = light_value.reshape(tok_rows, heads_here, head_size)
    token_position = jnp.arange(tok_rows)
    allowed = (code[:, None] == code[None, :]) & (token_position[None, :] <= token_position[:, None])
    decay_gap = jnp.where(allowed[None], decay_sum[:, :, None] - decay_sum[:, None, :], -jnp.inf)
    products = jnp.einsum("thd,shd->hts", query_heads, key_heads, preferred_element_type=F32)
    weights = (products * jnp.exp(decay_gap)).astype(BF16)
    mixed = jnp.einsum("hts,shd->thd", weights, value_heads, preferred_element_type=F32)
    to_end = jnp.where((code == code[-1])[None, :], jnp.exp(decay_sum[:, -1:] - decay_sum), 0.0)
    key_weighted = (key_heads * to_end.T[:, :, None]).astype(BF16)
    local_state = jnp.einsum("shd,she->hde", key_weighted, value_heads, preferred_element_type=F32)
    return mixed, local_state


def soft_window(soft_query, key_heads, value_heads, code, code_window, heads_here):
    tok_rows = soft_query.shape[0]
    kv_here, span, head_size = key_heads.shape
    group = heads_here // kv_here
    queries = soft_query.reshape(tok_rows, kv_here, group, head_size)
    key_position = jnp.arange(span)
    query_position = jnp.arange(tok_rows) + (span - tok_rows)
    allowed = (code[:, None] == code_window[None, :]) & (key_position[None, :] <= query_position[:, None])
    scores = jnp.einsum("tkgd,ksd->kgts", queries, key_heads, preferred_element_type=F32) * head_size ** (-0.5)
    scores = jnp.where(allowed, scores, NEG_BIG)
    row_max = jnp.max(scores, axis=-1)
    prob_block = jnp.exp(scores - row_max[..., None])
    row_total = jnp.sum(prob_block, axis=-1)
    weighted = jnp.einsum("kgts,ksd->kgtd", prob_block.astype(BF16), value_heads, preferred_element_type=F32)
    output = (weighted / row_total[..., None]).transpose(2, 0, 1, 3).reshape(tok_rows, heads_here * head_size)
    return output.astype(BF16)


def split_parts(value):
    high = lax.reduce_precision(value, exponent_bits=8, mantissa_bits=7)
    rest = value - high
    middle = lax.reduce_precision(rest, exponent_bits=8, mantissa_bits=7)
    return jnp.concatenate([high, middle, rest - middle])


def join_parts(parts):
    third = parts.shape[0] // 3
    parts = parts.astype(F32)
    return (parts[:third] + parts[third : 2 * third]) + parts[2 * third :]


def rows_of(flat, width):
    tile = 16 * width
    padded = -(-flat.shape[0] // tile) * tile
    return jnp.pad(flat, (0, padded - flat.shape[0])).reshape(-1, width).astype(BF16)


def on_device(
    light_query,
    light_key,
    light_value,
    light_gate,
    log_decay,
    norm_gain,
    soft_query,
    soft_key,
    soft_value,
    segment_ids,
):
    tok_rows = light_query.shape[0]
    heads_here = log_decay.shape[0]
    head_size = light_query.shape[1] // heads_here
    kv_here = soft_key.shape[1] // head_size
    assert -(-MAXDOC // tok_rows) == 4
    code = segment_ids.astype(F32) + 1.0
    decay_sum = jnp.cumsum(log_decay, axis=1)

    mixed, local_state = light_local(light_query, light_key, light_value, decay_sum, code)
    block_decay = jnp.exp(decay_sum[:, -1])

    own_keys = soft_key.reshape(tok_rows, kv_here, head_size).transpose(1, 0, 2)
    own_values = soft_value.reshape(tok_rows, kv_here, head_size).transpose(1, 0, 2)
    state_rows = heads_here * head_size
    kv_rows = kv_here * tok_rows
    own_state = local_state.astype(BF16)
    own_kv = jnp.concatenate(
        [
            own_keys.reshape(kv_rows, head_size),
            own_values.reshape(kv_rows, head_size),
            rows_of(jnp.concatenate([code, split_parts(block_decay)]), head_size),
        ]
    )
    state_1, kv_1 = shifted((own_state, own_kv), "ctx", 1)
    state_2, kv_2 = shifted((own_state, own_kv), "ctx", 2)

    def unpack(block):
        keys = block[:kv_rows].reshape(kv_here, tok_rows, head_size)
        values = block[kv_rows : 2 * kv_rows].reshape(kv_here, tok_rows, head_size)
        meta = block[2 * kv_rows :].reshape(-1)
        codes = meta[:tok_rows].astype(F32)
        decay = join_parts(meta[tok_rows : tok_rows + 3 * heads_here])
        return keys, values, codes, decay

    keys_1, values_1, code_1, decay_1 = unpack(kv_1)
    keys_2, values_2, code_2, decay_2 = unpack(kv_2)

    link_1 = (code_2[-1] == code_1[0]) & (code_1[0] == code_1[-1])
    pair_state = state_1.astype(F32) + jnp.where(link_1, decay_1, 0.0)[:, None, None] * state_2.astype(F32)

    relay_kv = jnp.concatenate([kv_2[: 2 * kv_rows], kv_1[: 2 * kv_rows], rows_of(jnp.concatenate([code_2, code_1]), head_size)])
    state_far, kv_far = shifted((pair_state.astype(BF16), relay_kv), "ctx", 2)
    state_far = state_far.astype(F32)
    keys_4 = kv_far[:kv_rows].reshape(kv_here, tok_rows, head_size)
    values_4 = kv_far[kv_rows : 2 * kv_rows].reshape(kv_here, tok_rows, head_size)
    keys_3 = kv_far[2 * kv_rows : 3 * kv_rows].reshape(kv_here, tok_rows, head_size)
    values_3 = kv_far[3 * kv_rows : 4 * kv_rows].reshape(kv_here, tok_rows, head_size)
    code_far = kv_far[4 * kv_rows :].reshape(-1)[: 2 * tok_rows].astype(F32)
    code_4, code_3 = code_far[:tok_rows], code_far[tok_rows:]

    link_2 = (code_3[-1] == code_2[0]) & (code_2[0] == code_1[-1])
    carry_scale = jnp.where(link_2, decay_2 * decay_1, 0.0)
    incoming_state = pair_state + carry_scale[:, None, None] * state_far

    query_heads = light_query.reshape(tok_rows, heads_here, head_size)
    carried_in = jnp.einsum(
        "thd,hde->the", query_heads.astype(F32), incoming_state, precision=lax.Precision.HIGHEST
    )
    uses_state = code == code_1[-1]
    scale_in = jnp.where(uses_state[None, :], jnp.exp(decay_sum), 0.0)
    mixed = mixed + carried_in * scale_in.T[:, :, None]
    squares = jnp.sum(mixed * mixed, axis=(1, 2))
    squares = lax.psum(squares, "tensor")
    features = heads_here * head_size * lax.axis_size("tensor")
    inverse = lax.rsqrt(squares / features + 1e-06)
    gate_open = jax.nn.sigmoid(light_gate.astype(F32)).reshape(tok_rows, heads_here, head_size)
    normed = mixed * inverse[:, None, None] * norm_gain.reshape(heads_here, head_size) * gate_open
    light_out = normed.reshape(tok_rows, heads_here * head_size).astype(BF16)

    key_window = jnp.concatenate([keys_4, keys_3, keys_2, keys_1, own_keys], axis=1)
    value_window = jnp.concatenate([values_4, values_3, values_2, values_1, own_values], axis=1)
    code_window = jnp.concatenate([code_4, code_3, code_2, code_1, code])
    soft_out = soft_window(soft_query, key_window, value_window, code, code_window, heads_here)
    return (light_out, soft_out)


def solution(mesh):
    in_specs = (
        P(("groups", "ctx"), "tensor"),
        P(("groups", "ctx"), "tensor"),
        P(("groups", "ctx"), "tensor"),
        P(("groups", "ctx"), "tensor"),
        P("tensor", ("groups", "ctx")),
        P("tensor"),
        P(("groups", "ctx"), "tensor"),
        P(("groups", "ctx"), "tensor"),
        P(("groups", "ctx"), "tensor"),
        P(("groups", "ctx")),
    )
    out_specs = (P(("groups", "ctx"), "tensor"), P(("groups", "ctx"), "tensor"))
    return jax.shard_map(
        on_device, mesh=mesh, in_specs=in_specs, out_specs=out_specs, check_vma=False
    )
```

```python
import jax
import jax.numpy as jnp
from jax import lax
from jax.experimental import pallas as pl
from jax.experimental.pallas import tpu as pltpu
from jax.sharding import PartitionSpec as P

NEG_BIG = -1e30
MAXDOC = 512
F32 = jnp.float32
BF16 = jnp.bfloat16


def shifted(block, axis, distance):
    devices = lax.axis_size(axis)
    route = [(i, i + distance) for i in range(devices - distance)]
    return lax.ppermute(block, axis, route)


def light_local(light_query, light_key, light_value, decay_sum, code):
    tok_rows, heads_here = light_query.shape[0], decay_sum.shape[0]
    head_size = light_query.shape[1] // heads_here
    query_heads = light_query.reshape(tok_rows, heads_here, head_size)
    key_heads = light_key.reshape(tok_rows, heads_here, head_size)
    value_heads = light_value.reshape(tok_rows, heads_here, head_size)
    token_position = jnp.arange(tok_rows)
    allowed = (code[:, None] == code[None, :]) & (token_position[None, :] <= token_position[:, None])
    decay_gap = jnp.where(allowed[None], decay_sum[:, :, None] - decay_sum[:, None, :], -jnp.inf)
    products = jnp.einsum("thd,shd->hts", query_heads, key_heads, preferred_element_type=F32)
    weights = (products * jnp.exp(decay_gap)).astype(BF16)
    mixed = jnp.einsum("hts,shd->thd", weights, value_heads, preferred_element_type=F32)
    return mixed


def state_kernel(decay_ref, code_ref, key_ref, value_ref, out_ref):
    heads_here, head_size = out_ref.shape[0], out_ref.shape[1]
    tok_rows = code_ref.shape[0]
    code = code_ref[...]
    same_end = code == code[tok_rows - 1 :, :]
    for head in range(heads_here):
        decay = decay_ref[:, head : head + 1]
        to_end = jnp.where(same_end, jnp.exp(decay[tok_rows - 1 :, :] - decay), 0.0)
        columns = slice(head * head_size, (head + 1) * head_size)
        weighted = (key_ref[:, columns].astype(F32) * to_end).T.astype(BF16)
        out_ref[head] = jnp.dot(weighted, value_ref[:, columns], preferred_element_type=F32).astype(BF16)


def local_state_of(decay_sum, code, light_key, light_value):
    heads_here = decay_sum.shape[0]
    head_size = light_key.shape[1] // heads_here
    tok_rows = light_key.shape[0]
    flops = 2 * heads_here * tok_rows * head_size * head_size
    return pl.pallas_call(
        state_kernel,
        out_shape=jax.ShapeDtypeStruct((heads_here, head_size, head_size), BF16),
        in_specs=[pl.BlockSpec(memory_space=pltpu.VMEM)] * 4,
        out_specs=pl.BlockSpec(memory_space=pltpu.VMEM),
        cost_estimate=pl.CostEstimate(flops=flops, bytes_accessed=3 * light_key.size, transcendentals=heads_here * tok_rows),
    )(decay_sum.T, code[:, None], light_key, light_value)


def soft_window(soft_query, key_heads, value_heads, code, code_window, heads_here):
    tok_rows = soft_query.shape[0]
    kv_here, span, head_size = key_heads.shape
    group = heads_here // kv_here
    queries = soft_query.reshape(tok_rows, kv_here, group, head_size)
    key_position = jnp.arange(span)
    query_position = jnp.arange(tok_rows) + (span - tok_rows)
    allowed = (code[:, None] == code_window[None, :]) & (key_position[None, :] <= query_position[:, None])
    scores = jnp.einsum("tkgd,ksd->kgts", queries, key_heads, preferred_element_type=F32) * head_size ** (-0.5)
    scores = jnp.where(allowed, scores, NEG_BIG)
    row_max = jnp.max(scores, axis=-1)
    prob_block = jnp.exp(scores - row_max[..., None])
    row_total = jnp.sum(prob_block, axis=-1)
    weighted = jnp.einsum("kgts,ksd->kgtd", prob_block.astype(BF16), value_heads, preferred_element_type=F32)
    output = (weighted / row_total[..., None]).transpose(2, 0, 1, 3).reshape(tok_rows, heads_here * head_size)
    return output.astype(BF16)


def split_parts(value):
    high = lax.reduce_precision(value, exponent_bits=8, mantissa_bits=7)
    rest = value - high
    middle = lax.reduce_precision(rest, exponent_bits=8, mantissa_bits=7)
    return jnp.concatenate([high, middle, rest - middle])


def join_parts(parts):
    third = parts.shape[0] // 3
    parts = parts.astype(F32)
    return (parts[:third] + parts[third : 2 * third]) + parts[2 * third :]


def rows_of(flat, width):
    tile = 16 * width
    padded = -(-flat.shape[0] // tile) * tile
    return jnp.pad(flat, (0, padded - flat.shape[0])).reshape(-1, width).astype(BF16)


def on_device(
    light_query,
    light_key,
    light_value,
    light_gate,
    log_decay,
    norm_gain,
    soft_query,
    soft_key,
    soft_value,
    segment_ids,
):
    tok_rows = light_query.shape[0]
    heads_here = log_decay.shape[0]
    head_size = light_query.shape[1] // heads_here
    kv_here = soft_key.shape[1] // head_size
    assert -(-MAXDOC // tok_rows) == 4
    code = segment_ids.astype(F32) + 1.0
    decay_sum = jnp.cumsum(log_decay, axis=1)

    own_state = local_state_of(decay_sum, code, light_key, light_value)
    mixed = light_local(light_query, light_key, light_value, decay_sum, code)
    block_decay = jnp.exp(decay_sum[:, -1])

    own_keys = soft_key.reshape(tok_rows, kv_here, head_size).transpose(1, 0, 2)
    own_values = soft_value.reshape(tok_rows, kv_here, head_size).transpose(1, 0, 2)
    state_rows = heads_here * head_size
    kv_rows = kv_here * tok_rows
    own_kv = jnp.concatenate(
        [
            own_keys.reshape(kv_rows, head_size),
            own_values.reshape(kv_rows, head_size),
            rows_of(jnp.concatenate([code, split_parts(block_decay)]), head_size),
        ]
    )
    state_1, kv_1 = shifted((own_state, own_kv), "ctx", 1)
    state_2, kv_2 = shifted((own_state, own_kv), "ctx", 2)

    def unpack(block):
        keys = block[:kv_rows].reshape(kv_here, tok_rows, head_size)
        values = block[kv_rows : 2 * kv_rows].reshape(kv_here, tok_rows, head_size)
        meta = block[2 * kv_rows :].reshape(-1)
        codes = meta[:tok_rows].astype(F32)
        decay = join_parts(meta[tok_rows : tok_rows + 3 * heads_here])
        return keys, values, codes, decay

    keys_1, values_1, code_1, decay_1 = unpack(kv_1)
    keys_2, values_2, code_2, decay_2 = unpack(kv_2)

    link_1 = (code_2[-1] == code_1[0]) & (code_1[0] == code_1[-1])
    pair_state = state_1.astype(F32) + jnp.where(link_1, decay_1, 0.0)[:, None, None] * state_2.astype(F32)

    relay_kv = jnp.concatenate([kv_2[: 2 * kv_rows], kv_1[: 2 * kv_rows], rows_of(jnp.concatenate([code_2, code_1]), head_size)])
    state_far, kv_far = shifted((pair_state.astype(BF16), relay_kv), "ctx", 2)
    state_far = state_far.astype(F32)
    keys_4 = kv_far[:kv_rows].reshape(kv_here, tok_rows, head_size)
    values_4 = kv_far[kv_rows : 2 * kv_rows].reshape(kv_here, tok_rows, head_size)
    keys_3 = kv_far[2 * kv_rows : 3 * kv_rows].reshape(kv_here, tok_rows, head_size)
    values_3 = kv_far[3 * kv_rows : 4 * kv_rows].reshape(kv_here, tok_rows, head_size)
    code_far = kv_far[4 * kv_rows :].reshape(-1)[: 2 * tok_rows].astype(F32)
    code_4, code_3 = code_far[:tok_rows], code_far[tok_rows:]

    link_2 = (code_3[-1] == code_2[0]) & (code_2[0] == code_1[-1])
    carry_scale = jnp.where(link_2, decay_2 * decay_1, 0.0)
    incoming_state = pair_state + carry_scale[:, None, None] * state_far

    query_heads = light_query.reshape(tok_rows, heads_here, head_size)
    carried_in = jnp.einsum(
        "thd,hde->the", query_heads.astype(F32), incoming_state, precision=lax.Precision.HIGHEST
    )
    uses_state = code == code_1[-1]
    scale_in = jnp.where(uses_state[None, :], jnp.exp(decay_sum), 0.0)
    mixed = mixed + carried_in * scale_in.T[:, :, None]
    squares = jnp.sum(mixed * mixed, axis=(1, 2))
    squares = lax.psum(squares, "tensor")
    features = heads_here * head_size * lax.axis_size("tensor")
    inverse = lax.rsqrt(squares / features + 1e-06)
    gate_open = jax.nn.sigmoid(light_gate.astype(F32)).reshape(tok_rows, heads_here, head_size)
    normed = mixed * inverse[:, None, None] * norm_gain.reshape(heads_here, head_size) * gate_open
    light_out = normed.reshape(tok_rows, heads_here * head_size).astype(BF16)

    key_window = jnp.concatenate([keys_4, keys_3, keys_2, keys_1, own_keys], axis=1)
    value_window = jnp.concatenate([values_4, values_3, values_2, values_1, own_values], axis=1)
    code_window = jnp.concatenate([code_4, code_3, code_2, code_1, code])
    soft_out = soft_window(soft_query, key_window, value_window, code, code_window, heads_here)
    return (light_out, soft_out)


def solution(mesh):
    in_specs = (
        P(("groups", "ctx"), "tensor"),
        P(("groups", "ctx"), "tensor"),
        P(("groups", "ctx"), "tensor"),
        P(("groups", "ctx"), "tensor"),
        P("tensor", ("groups", "ctx")),
        P("tensor"),
        P(("groups", "ctx"), "tensor"),
        P(("groups", "ctx"), "tensor"),
        P(("groups", "ctx"), "tensor"),
        P(("groups", "ctx")),
    )
    out_specs = (P(("groups", "ctx"), "tensor"), P(("groups", "ctx"), "tensor"))
    return jax.shard_map(
        on_device, mesh=mesh, in_specs=in_specs, out_specs=out_specs, check_vma=False
    )
```

```python
import jax
import jax.numpy as jnp
from jax import lax
from jax.experimental import pallas as pl
from jax.experimental.pallas import tpu as pltpu
from jax.sharding import PartitionSpec as P


NEG_BIG = -1e30
MAXDOC = 512
F32 = jnp.float32
BF16 = jnp.bfloat16


def shifted(block, axis, distance):
    devices = lax.axis_size(axis)
    route = [(i, i + distance) for i in range(devices - distance)]
    return lax.ppermute(block, axis, route)


def light_local(light_query, light_key, light_value, decay_sum, code):
    tok_rows, heads_here = light_query.shape[0], decay_sum.shape[0]
    head_size = light_query.shape[1] // heads_here
    query_heads = light_query.reshape(tok_rows, heads_here, head_size)
    key_heads = light_key.reshape(tok_rows, heads_here, head_size)
    value_heads = light_value.reshape(tok_rows, heads_here, head_size)
    token_position = jnp.arange(tok_rows)
    allowed = (code[:, None] == code[None, :]) & (token_position[None, :] <= token_position[:, None])
    decay_gap = jnp.where(allowed[None], decay_sum[:, :, None] - decay_sum[:, None, :], -jnp.inf)
    products = jnp.einsum("thd,shd->hts", query_heads, key_heads, preferred_element_type=F32)
    weights = (products * jnp.exp(decay_gap)).astype(BF16)
    mixed = jnp.einsum("hts,shd->thd", weights, value_heads, preferred_element_type=F32)
    return mixed


def state_kernel(decay_ref, code_ref, key_ref, value_ref, out_ref):
    heads_here, head_size = out_ref.shape[0], out_ref.shape[1]
    tok_rows = code_ref.shape[0]
    code = code_ref[...]
    same_end = code == code[tok_rows - 1 :, :]
    for head in range(heads_here):
        decay = decay_ref[:, head : head + 1]
        to_end = jnp.where(same_end, jnp.exp(decay[tok_rows - 1 :, :] - decay), 0.0)
        columns = slice(head * head_size, (head + 1) * head_size)
        weighted = (key_ref[:, columns].astype(F32) * to_end).T.astype(BF16)
        out_ref[head] = jnp.dot(weighted, value_ref[:, columns], preferred_element_type=F32).astype(BF16)


def local_state_of(decay_sum, code, light_key, light_value):
    heads_here = decay_sum.shape[0]
    head_size = light_key.shape[1] // heads_here
    tok_rows = light_key.shape[0]
    flops = 2 * heads_here * tok_rows * head_size * head_size
    return pl.pallas_call(
        state_kernel,
        out_shape=jax.ShapeDtypeStruct((heads_here, head_size, head_size), BF16),
        in_specs=[pl.BlockSpec(memory_space=pltpu.VMEM)] * 4,
        out_specs=pl.BlockSpec(memory_space=pltpu.VMEM),
        cost_estimate=pl.CostEstimate(flops=flops, bytes_accessed=3 * light_key.size, transcendentals=heads_here * tok_rows),
    )(decay_sum.T, code[:, None], light_key, light_value)


def soft_window(soft_query, key_heads, value_heads, code, code_window, heads_here):
    tok_rows = soft_query.shape[0]
    kv_here, span, head_size = key_heads.shape
    group = heads_here // kv_here
    queries = soft_query.reshape(tok_rows, kv_here, group, head_size)
    key_position = jnp.arange(span)
    query_position = jnp.arange(tok_rows) + (span - tok_rows)
    allowed = (code[:, None] == code_window[None, :]) & (key_position[None, :] <= query_position[:, None])
    scores = jnp.einsum("tkgd,ksd->kgts", queries, key_heads, preferred_element_type=F32) * head_size ** (-0.5)
    scores = jnp.where(allowed, scores, NEG_BIG)
    row_max = jnp.max(scores, axis=-1)
    prob_block = jnp.exp(scores - row_max[..., None])
    row_total = jnp.sum(prob_block, axis=-1)
    weighted = jnp.einsum("kgts,ksd->kgtd", prob_block.astype(BF16), value_heads, preferred_element_type=F32)
    output = (weighted / row_total[..., None]).transpose(2, 0, 1, 3).reshape(tok_rows, heads_here * head_size)
    return output.astype(BF16)


def split_parts(value):
    high = lax.reduce_precision(value, exponent_bits=8, mantissa_bits=7)
    rest = value - high
    middle = lax.reduce_precision(rest, exponent_bits=8, mantissa_bits=7)
    return jnp.concatenate([high, middle, rest - middle])


def join_parts(parts):
    third = parts.shape[0] // 3
    parts = parts.astype(F32)
    return (parts[:third] + parts[third : 2 * third]) + parts[2 * third :]


def rows_of(flat, width):
    tile = 16 * width
    padded = -(-flat.shape[0] // tile) * tile
    return jnp.pad(flat, (0, padded - flat.shape[0])).reshape(-1, width).astype(BF16)


def on_device_body(
    light_query,
    light_key,
    light_value,
    light_gate,
    log_decay,
    norm_gain,
    soft_query,
    soft_key,
    soft_value,
    segment_ids,
):
    tok_rows = light_query.shape[0]
    heads_here = log_decay.shape[0]
    head_size = light_query.shape[1] // heads_here
    kv_here = soft_key.shape[1] // head_size
    assert -(-MAXDOC // tok_rows) == 4
    code = segment_ids.astype(F32) + 1.0
    decay_sum = jnp.cumsum(log_decay, axis=1)

    own_state = local_state_of(decay_sum, code, light_key, light_value)
    mixed = light_local(light_query, light_key, light_value, decay_sum, code)
    block_decay = jnp.exp(decay_sum[:, -1])

    own_keys = soft_key.reshape(tok_rows, kv_here, head_size).transpose(1, 0, 2)
    own_values = soft_value.reshape(tok_rows, kv_here, head_size).transpose(1, 0, 2)
    kv_rows = kv_here * tok_rows
    own_kv = jnp.concatenate(
        [
            own_keys.reshape(kv_rows, head_size),
            own_values.reshape(kv_rows, head_size),
            rows_of(jnp.concatenate([code, split_parts(block_decay)]), head_size),
        ]
    )
    state_1 = shifted(own_state, "ctx", 1)
    state_2 = shifted(own_state, "ctx", 2)
    kv_1 = shifted(own_kv, "ctx", 1)
    kv_2 = shifted(own_kv, "ctx", 2)

    def unpack(block):
        keys = block[:kv_rows].reshape(kv_here, tok_rows, head_size)
        values = block[kv_rows : 2 * kv_rows].reshape(kv_here, tok_rows, head_size)
        meta = block[2 * kv_rows :].reshape(-1)
        codes = meta[:tok_rows].astype(F32)
        decay = join_parts(meta[tok_rows : tok_rows + 3 * heads_here])
        return keys, values, codes, decay

    keys_1, values_1, code_1, decay_1 = unpack(kv_1)
    keys_2, values_2, code_2, decay_2 = unpack(kv_2)

    link_1 = (code_2[-1] == code_1[0]) & (code_1[0] == code_1[-1])
    pair_state = state_1.astype(F32) + jnp.where(link_1, decay_1, 0.0)[:, None, None] * state_2.astype(F32)

    relay_kv = jnp.concatenate([kv_2[: 2 * kv_rows], kv_1[: 2 * kv_rows], rows_of(jnp.concatenate([code_2, code_1]), head_size)])
    state_far = shifted(pair_state.astype(BF16), "ctx", 2)
    kv_far = shifted(relay_kv, "ctx", 2)
    state_far = state_far.astype(F32)
    keys_4 = kv_far[:kv_rows].reshape(kv_here, tok_rows, head_size)
    values_4 = kv_far[kv_rows : 2 * kv_rows].reshape(kv_here, tok_rows, head_size)
    keys_3 = kv_far[2 * kv_rows : 3 * kv_rows].reshape(kv_here, tok_rows, head_size)
    values_3 = kv_far[3 * kv_rows : 4 * kv_rows].reshape(kv_here, tok_rows, head_size)
    code_far = kv_far[4 * kv_rows :].reshape(-1)[: 2 * tok_rows].astype(F32)
    code_4, code_3 = code_far[:tok_rows], code_far[tok_rows:]

    link_2 = (code_3[-1] == code_2[0]) & (code_2[0] == code_1[-1])
    carry_scale = jnp.where(link_2, decay_2 * decay_1, 0.0)
    incoming_state = pair_state + carry_scale[:, None, None] * state_far

    query_heads = light_query.reshape(tok_rows, heads_here, head_size)
    carried_in = jnp.einsum(
        "thd,hde->the", query_heads.astype(F32), incoming_state, precision=lax.Precision.HIGHEST
    )
    uses_state = code == code_1[-1]
    scale_in = jnp.where(uses_state[None, :], jnp.exp(decay_sum), 0.0)
    mixed = mixed + carried_in * scale_in.T[:, :, None]
    squares = jnp.sum(mixed * mixed, axis=(1, 2))
    squares = lax.psum(squares, "tensor")
    features = heads_here * head_size * lax.axis_size("tensor")
    inverse = lax.rsqrt(squares / features + 1e-06)
    gate_open = jax.nn.sigmoid(light_gate.astype(F32)).reshape(tok_rows, heads_here, head_size)
    normed = mixed * inverse[:, None, None] * norm_gain.reshape(heads_here, head_size) * gate_open
    light_out = normed.reshape(tok_rows, heads_here * head_size).astype(BF16)

    key_window = jnp.concatenate([keys_4, keys_3, keys_2, keys_1, own_keys], axis=1)
    value_window = jnp.concatenate([values_4, values_3, values_2, values_1, own_values], axis=1)
    code_window = jnp.concatenate([code_4, code_3, code_2, code_1, code])
    soft_out = soft_window(soft_query, key_window, value_window, code, code_window, heads_here)
    return (light_out, soft_out)


def solution(mesh):
    in_specs = (
        P(("groups", "ctx"), "tensor"),
        P(("groups", "ctx"), "tensor"),
        P(("groups", "ctx"), "tensor"),
        P(("groups", "ctx"), "tensor"),
        P("tensor", ("groups", "ctx")),
        P("tensor"),
        P(("groups", "ctx"), "tensor"),
        P(("groups", "ctx"), "tensor"),
        P(("groups", "ctx"), "tensor"),
        P(("groups", "ctx")),
    )
    out_specs = (P(("groups", "ctx"), "tensor"), P(("groups", "ctx"), "tensor"))
    return jax.shard_map(on_device_body, mesh=mesh, in_specs=in_specs, out_specs=out_specs, check_vma=False)
```

```python
import jax
import jax.numpy as jnp
from jax import lax
from jax.experimental import pallas as pl
from jax.experimental.pallas import tpu as pltpu
from jax.sharding import PartitionSpec as P

NEG_BIG = -1e30
MAXDOC = 512
F32 = jnp.float32
BF16 = jnp.bfloat16


def shifted(block, axis, distance):
    devices = lax.axis_size(axis)
    route = [(i, i + distance) for i in range(devices - distance)]
    return lax.ppermute(block, axis, route)


def light_local(light_query, light_key, light_value, decay_sum, code):
    tok_rows, heads_here = light_query.shape[0], decay_sum.shape[0]
    head_size = light_query.shape[1] // heads_here
    query_heads = light_query.reshape(tok_rows, heads_here, head_size)
    key_heads = light_key.reshape(tok_rows, heads_here, head_size)
    value_heads = light_value.reshape(tok_rows, heads_here, head_size)
    token_position = jnp.arange(tok_rows)
    allowed = (code[:, None] == code[None, :]) & (token_position[None, :] <= token_position[:, None])
    decay_gap = jnp.where(allowed[None], decay_sum[:, :, None] - decay_sum[:, None, :], -jnp.inf)
    products = jnp.einsum("thd,shd->hts", query_heads, key_heads, preferred_element_type=F32)
    weights = (products * jnp.exp(decay_gap)).astype(BF16)
    mixed = jnp.einsum("hts,shd->thd", weights, value_heads, preferred_element_type=F32)
    return mixed


def state_kernel(decay_ref, code_ref, key_ref, value_ref, out_ref):
    heads_here, head_size = out_ref.shape[0], out_ref.shape[1]
    tok_rows = code_ref.shape[0]
    code = code_ref[...]
    same_end = code == code[tok_rows - 1 :, :]
    for head in range(heads_here):
        decay = decay_ref[:, head : head + 1]
        to_end = jnp.where(same_end, jnp.exp(decay[tok_rows - 1 :, :] - decay), 0.0)
        columns = slice(head * head_size, (head + 1) * head_size)
        weighted = (key_ref[:, columns].astype(F32) * to_end).T.astype(BF16)
        out_ref[head] = jnp.dot(weighted, value_ref[:, columns], preferred_element_type=F32).astype(BF16)


def local_state_of(decay_sum, code, light_key, light_value):
    heads_here = decay_sum.shape[0]
    head_size = light_key.shape[1] // heads_here
    tok_rows = light_key.shape[0]
    flops = 2 * heads_here * tok_rows * head_size * head_size
    return pl.pallas_call(
        state_kernel,
        out_shape=jax.ShapeDtypeStruct((heads_here, head_size, head_size), BF16),
        in_specs=[pl.BlockSpec(memory_space=pltpu.VMEM)] * 4,
        out_specs=pl.BlockSpec(memory_space=pltpu.VMEM),
        cost_estimate=pl.CostEstimate(flops=flops, bytes_accessed=3 * light_key.size, transcendentals=heads_here * tok_rows),
    )(decay_sum.T, code[:, None], light_key, light_value)


def intra_kernel(decay_ref, decay_t_ref, code_row_ref, code_col_ref, query_ref, key_ref, value_ref, out_ref):
    heads_here = decay_ref.shape[0]
    tok_rows = code_col_ref.shape[0]
    head_size = query_ref.shape[1] // heads_here
    rows = lax.broadcasted_iota(jnp.int32, (tok_rows, tok_rows), 0)
    cols = lax.broadcasted_iota(jnp.int32, (tok_rows, tok_rows), 1)
    allowed = (code_col_ref[...] == code_row_ref[...]) & (cols <= rows)
    for head in range(heads_here):
        columns = slice(head * head_size, (head + 1) * head_size)
        gap = jnp.where(allowed, decay_t_ref[:, head : head + 1] - decay_ref[head : head + 1, :], -jnp.inf)
        products = lax.dot_general(
            query_ref[:, columns], key_ref[:, columns], (((1,), (1,)), ((), ())), preferred_element_type=F32
        )
        weights = (products * jnp.exp(gap)).astype(BF16)
        out_ref[:, columns] = jnp.dot(weights, value_ref[:, columns], preferred_element_type=F32)


def intra_mixed(decay_sum, code, light_query, light_key, light_value):
    heads_here = decay_sum.shape[0]
    tok_rows, width = light_query.shape
    flops = 4 * tok_rows * tok_rows * width
    return pl.pallas_call(
        intra_kernel,
        out_shape=jax.ShapeDtypeStruct((tok_rows, width), F32),
        in_specs=[pl.BlockSpec(memory_space=pltpu.VMEM)] * 7,
        out_specs=pl.BlockSpec(memory_space=pltpu.VMEM),
        cost_estimate=pl.CostEstimate(flops=flops, bytes_accessed=10 * light_query.size, transcendentals=heads_here * tok_rows * tok_rows),
    )(decay_sum, decay_sum.T, code[None, :], code[:, None], light_query, light_key, light_value)


def final_kernel(carry_ref, scale_t_ref, query_ref, mixed_ref, pair_ref, far_ref, out_ref, squares_ref):
    heads_here, head_size = pair_ref.shape[0], pair_ref.shape[1]
    squares = jnp.zeros((query_ref.shape[0], 1), F32)
    for head in range(heads_here):
        columns = slice(head * head_size, (head + 1) * head_size)
        state = pair_ref[head] + carry_ref[head] * far_ref[head].astype(F32)
        carried = jnp.dot(
            query_ref[:, columns].astype(F32), state, precision=lax.Precision.HIGHEST, preferred_element_type=F32
        )
        total = mixed_ref[:, columns] + carried * scale_t_ref[:, head : head + 1]
        out_ref[:, columns] = total
        squares = squares + jnp.sum(total * total, axis=1, keepdims=True)
    squares_ref[...] = squares


def final_mixed(carry_scale, scale_in, light_query, mixed, pair_state, state_far):
    tok_rows, width = light_query.shape
    heads_here = pair_state.shape[0]
    flops = 12 * tok_rows * width * pair_state.shape[1]
    return pl.pallas_call(
        final_kernel,
        out_shape=(jax.ShapeDtypeStruct((tok_rows, width), F32), jax.ShapeDtypeStruct((tok_rows, 1), F32)),
        in_specs=[pl.BlockSpec(memory_space=pltpu.SMEM)] + [pl.BlockSpec(memory_space=pltpu.VMEM)] * 5,
        out_specs=(pl.BlockSpec(memory_space=pltpu.VMEM), pl.BlockSpec(memory_space=pltpu.VMEM)),
        cost_estimate=pl.CostEstimate(flops=flops, bytes_accessed=4 * mixed.size * 3, transcendentals=0),
    )(carry_scale, scale_in.T, light_query, mixed, pair_state, state_far)


def soft_window(soft_query, key_heads, value_heads, code, code_window, heads_here):
    tok_rows = soft_query.shape[0]
    kv_here, span, head_size = key_heads.shape
    group = heads_here // kv_here
    queries = soft_query.reshape(tok_rows, kv_here, group, head_size)
    key_position = jnp.arange(span)
    query_position = jnp.arange(tok_rows) + (span - tok_rows)
    allowed = (code[:, None] == code_window[None, :]) & (key_position[None, :] <= query_position[:, None])
    scores = jnp.einsum("tkgd,ksd->kgts", queries, key_heads, preferred_element_type=F32) * head_size ** (-0.5)
    scores = jnp.where(allowed, scores, NEG_BIG)
    row_max = jnp.max(scores, axis=-1)
    prob_block = jnp.exp(scores - row_max[..., None])
    row_total = jnp.sum(prob_block, axis=-1)
    weighted = jnp.einsum("kgts,ksd->kgtd", prob_block.astype(BF16), value_heads, preferred_element_type=F32)
    output = (weighted / row_total[..., None]).transpose(2, 0, 1, 3).reshape(tok_rows, heads_here * head_size)
    return output.astype(BF16)


def split_parts(value):
    high = lax.reduce_precision(value, exponent_bits=8, mantissa_bits=7)
    rest = value - high
    middle = lax.reduce_precision(rest, exponent_bits=8, mantissa_bits=7)
    return jnp.concatenate([high, middle, rest - middle])


def join_parts(parts):
    third = parts.shape[0] // 3
    parts = parts.astype(F32)
    return (parts[:third] + parts[third : 2 * third]) + parts[2 * third :]


def rows_of(flat, width):
    tile = 16 * width
    padded = -(-flat.shape[0] // tile) * tile
    return jnp.pad(flat, (0, padded - flat.shape[0])).reshape(-1, width).astype(BF16)


def on_device(
    light_query,
    light_key,
    light_value,
    light_gate,
    log_decay,
    norm_gain,
    soft_query,
    soft_key,
    soft_value,
    segment_ids,
):
    tok_rows = light_query.shape[0]
    heads_here = log_decay.shape[0]
    head_size = light_query.shape[1] // heads_here
    kv_here = soft_key.shape[1] // head_size
    assert -(-MAXDOC // tok_rows) == 4
    code = segment_ids.astype(F32) + 1.0
    decay_sum = jnp.cumsum(log_decay, axis=1)

    own_state = local_state_of(decay_sum, code, light_key, light_value)
    mixed = intra_mixed(decay_sum, code, light_query, light_key, light_value)
    block_decay = jnp.exp(decay_sum[:, -1])

    own_keys = soft_key.reshape(tok_rows, kv_here, head_size).transpose(1, 0, 2)
    own_values = soft_value.reshape(tok_rows, kv_here, head_size).transpose(1, 0, 2)
    state_rows = heads_here * head_size
    kv_rows = kv_here * tok_rows
    own_kv = jnp.concatenate(
        [
            own_keys.reshape(kv_rows, head_size),
            own_values.reshape(kv_rows, head_size),
            rows_of(jnp.concatenate([code, split_parts(block_decay)]), head_size),
        ]
    )
    state_1, kv_1 = shifted((own_state, own_kv), "ctx", 1)
    state_2, kv_2 = shifted((own_state, own_kv), "ctx", 2)

    def unpack(block):
        keys = block[:kv_rows].reshape(kv_here, tok_rows, head_size)
        values = block[kv_rows : 2 * kv_rows].reshape(kv_here, tok_rows, head_size)
        meta = block[2 * kv_rows :].reshape(-1)
        codes = meta[:tok_rows].astype(F32)
        decay = join_parts(meta[tok_rows : tok_rows + 3 * heads_here])
        return keys, values, codes, decay

    keys_1, values_1, code_1, decay_1 = unpack(kv_1)
    keys_2, values_2, code_2, decay_2 = unpack(kv_2)

    link_1 = (code_2[-1] == code_1[0]) & (code_1[0] == code_1[-1])
    pair_state = state_1.astype(F32) + jnp.where(link_1, decay_1, 0.0)[:, None, None] * state_2.astype(F32)

    relay_kv = jnp.concatenate([kv_2[: 2 * kv_rows], kv_1[: 2 * kv_rows], rows_of(jnp.concatenate([code_2, code_1]), head_size)])
    state_far, kv_far = shifted((pair_state.astype(BF16), relay_kv), "ctx", 2)
    keys_4 = kv_far[:kv_rows].reshape(kv_here, tok_rows, head_size)
    values_4 = kv_far[kv_rows : 2 * kv_rows].reshape(kv_here, tok_rows, head_size)
    keys_3 = kv_far[2 * kv_rows : 3 * kv_rows].reshape(kv_here, tok_rows, head_size)
    values_3 = kv_far[3 * kv_rows : 4 * kv_rows].reshape(kv_here, tok_rows, head_size)
    code_far = kv_far[4 * kv_rows :].reshape(-1)[: 2 * tok_rows].astype(F32)
    code_4, code_3 = code_far[:tok_rows], code_far[tok_rows:]

    link_2 = (code_3[-1] == code_2[0]) & (code_2[0] == code_1[-1])
    carry_scale = jnp.where(link_2, decay_2 * decay_1, 0.0)
    uses_state = code == code_1[-1]
    scale_in = jnp.where(uses_state[None, :], jnp.exp(decay_sum), 0.0)
    mixed, squares = final_mixed(carry_scale, scale_in, light_query, mixed, pair_state, state_far)
    mixed = mixed.reshape(tok_rows, heads_here, head_size)
    squares = lax.psum(squares[:, 0], "tensor")
    features = heads_here * head_size * lax.axis_size("tensor")
    inverse = lax.rsqrt(squares / features + 1e-06)
    gate_open = jax.nn.sigmoid(light_gate.astype(F32)).reshape(tok_rows, heads_here, head_size)
    normed = mixed * inverse[:, None, None] * norm_gain.reshape(heads_here, head_size) * gate_open
    light_out = normed.reshape(tok_rows, heads_here * head_size).astype(BF16)

    key_window = jnp.concatenate([keys_4, keys_3, keys_2, keys_1, own_keys], axis=1)
    value_window = jnp.concatenate([values_4, values_3, values_2, values_1, own_values], axis=1)
    code_window = jnp.concatenate([code_4, code_3, code_2, code_1, code])
    soft_out = soft_window(soft_query, key_window, value_window, code, code_window, heads_here)
    return (light_out, soft_out)


def solution(mesh):
    in_specs = (
        P(("groups", "ctx"), "tensor"),
        P(("groups", "ctx"), "tensor"),
        P(("groups", "ctx"), "tensor"),
        P(("groups", "ctx"), "tensor"),
        P("tensor", ("groups", "ctx")),
        P("tensor"),
        P(("groups", "ctx"), "tensor"),
        P(("groups", "ctx"), "tensor"),
        P(("groups", "ctx"), "tensor"),
        P(("groups", "ctx")),
    )
    out_specs = (P(("groups", "ctx"), "tensor"), P(("groups", "ctx"), "tensor"))
    return jax.shard_map(
        on_device, mesh=mesh, in_specs=in_specs, out_specs=out_specs, check_vma=False
    )
```

```python
import jax
import jax.numpy as jnp
from jax import lax
from jax.experimental import pallas as pl
from jax.experimental.pallas import tpu as pltpu
from jax.sharding import PartitionSpec as P


NEG_BIG = -1e30
MAXDOC = 512
F32 = jnp.float32
BF16 = jnp.bfloat16


def shifted(block, axis, distance):
    devices = lax.axis_size(axis)
    route = [(i, i + distance) for i in range(devices - distance)]
    return lax.ppermute(block, axis, route)


def state_kernel(decay_ref, code_ref, key_ref, value_ref, out_ref):
    heads_here, head_size = out_ref.shape[0], out_ref.shape[1]
    tok_rows = code_ref.shape[0]
    code = code_ref[...]
    same_end = code == code[tok_rows - 1 :, :]
    for head in range(heads_here):
        decay = decay_ref[:, head : head + 1]
        to_end = jnp.where(same_end, jnp.exp(decay[tok_rows - 1 :, :] - decay), 0.0)
        columns = slice(head * head_size, (head + 1) * head_size)
        weighted = (key_ref[:, columns].astype(F32) * to_end).T.astype(BF16)
        out_ref[head] = jnp.dot(weighted, value_ref[:, columns], preferred_element_type=F32).astype(BF16)


def local_state_of(decay_sum, code, light_key, light_value):
    heads_here = decay_sum.shape[0]
    head_size = light_key.shape[1] // heads_here
    tok_rows = light_key.shape[0]
    flops = 2 * heads_here * tok_rows * head_size * head_size
    return pl.pallas_call(
        state_kernel,
        out_shape=jax.ShapeDtypeStruct((heads_here, head_size, head_size), BF16),
        in_specs=[pl.BlockSpec(memory_space=pltpu.VMEM)] * 4,
        out_specs=pl.BlockSpec(memory_space=pltpu.VMEM),
        cost_estimate=pl.CostEstimate(flops=flops, bytes_accessed=3 * light_key.size, transcendentals=heads_here * tok_rows),
    )(decay_sum.T, code[:, None], light_key, light_value)


def intra_kernel(decay_ref, decay_t_ref, code_row_ref, code_col_ref, query_ref, key_ref, value_ref, out_ref):
    heads_here = decay_ref.shape[0]
    tok_rows = code_col_ref.shape[0]
    head_size = query_ref.shape[1] // heads_here
    rows = lax.broadcasted_iota(jnp.int32, (tok_rows, tok_rows), 0)
    cols = lax.broadcasted_iota(jnp.int32, (tok_rows, tok_rows), 1)
    allowed = (code_col_ref[...] == code_row_ref[...]) & (cols <= rows)
    for head in range(heads_here):
        columns = slice(head * head_size, (head + 1) * head_size)
        gap = jnp.where(allowed, decay_t_ref[:, head : head + 1] - decay_ref[head : head + 1, :], -jnp.inf)
        products = lax.dot_general(
            query_ref[:, columns], key_ref[:, columns], (((1,), (1,)), ((), ())), preferred_element_type=F32
        )
        weights = (products * jnp.exp(gap)).astype(BF16)
        out_ref[:, columns] = jnp.dot(weights, value_ref[:, columns], preferred_element_type=F32)


def intra_mixed(decay_sum, code, light_query, light_key, light_value):
    heads_here = decay_sum.shape[0]
    tok_rows, width = light_query.shape
    flops = 4 * tok_rows * tok_rows * width
    return pl.pallas_call(
        intra_kernel,
        out_shape=jax.ShapeDtypeStruct((tok_rows, width), F32),
        in_specs=[pl.BlockSpec(memory_space=pltpu.VMEM)] * 7,
        out_specs=pl.BlockSpec(memory_space=pltpu.VMEM),
        cost_estimate=pl.CostEstimate(flops=flops, bytes_accessed=10 * light_query.size, transcendentals=heads_here * tok_rows * tok_rows),
    )(decay_sum, decay_sum.T, code[None, :], code[:, None], light_query, light_key, light_value)


def final_kernel(carry_ref, scale_t_ref, query_ref, mixed_ref, pair_ref, far_ref, out_ref, squares_ref):
    heads_here, head_size = pair_ref.shape[0], pair_ref.shape[1]
    squares = jnp.zeros((query_ref.shape[0], 1), F32)
    for head in range(heads_here):
        columns = slice(head * head_size, (head + 1) * head_size)
        state = pair_ref[head] + carry_ref[head] * far_ref[head].astype(F32)
        carried = jnp.dot(
            query_ref[:, columns].astype(F32), state, precision=lax.Precision.HIGHEST, preferred_element_type=F32
        )
        total = mixed_ref[:, columns] + carried * scale_t_ref[:, head : head + 1]
        out_ref[:, columns] = total
        squares = squares + jnp.sum(total * total, axis=1, keepdims=True)
    squares_ref[...] = squares


def final_mixed(carry_scale, scale_in, light_query, mixed, pair_state, state_far):
    tok_rows, width = light_query.shape
    flops = 12 * tok_rows * width * pair_state.shape[1]
    return pl.pallas_call(
        final_kernel,
        out_shape=(jax.ShapeDtypeStruct((tok_rows, width), F32), jax.ShapeDtypeStruct((tok_rows, 1), F32)),
        in_specs=[pl.BlockSpec(memory_space=pltpu.SMEM)] + [pl.BlockSpec(memory_space=pltpu.VMEM)] * 5,
        out_specs=(pl.BlockSpec(memory_space=pltpu.VMEM), pl.BlockSpec(memory_space=pltpu.VMEM)),
        cost_estimate=pl.CostEstimate(flops=flops, bytes_accessed=4 * mixed.size * 3, transcendentals=0),
    )(carry_scale, scale_in.T, light_query, mixed, pair_state, state_far)


def soft_window(soft_query, key_heads, value_heads, code, code_window, heads_here):
    tok_rows = soft_query.shape[0]
    kv_here, span, head_size = key_heads.shape
    group = heads_here // kv_here
    queries = soft_query.reshape(tok_rows, kv_here, group, head_size)
    key_position = jnp.arange(span)
    query_position = jnp.arange(tok_rows) + (span - tok_rows)
    allowed = (code[:, None] == code_window[None, :]) & (key_position[None, :] <= query_position[:, None])
    scores = jnp.einsum("tkgd,ksd->kgts", queries, key_heads, preferred_element_type=F32) * head_size ** (-0.5)
    scores = jnp.where(allowed, scores, NEG_BIG)
    row_max = jnp.max(scores, axis=-1)
    prob_block = jnp.exp(scores - row_max[..., None])
    row_total = jnp.sum(prob_block, axis=-1)
    weighted = jnp.einsum("kgts,ksd->kgtd", prob_block.astype(BF16), value_heads, preferred_element_type=F32)
    output = (weighted / row_total[..., None]).transpose(2, 0, 1, 3).reshape(tok_rows, heads_here * head_size)
    return output.astype(BF16)


def split_parts(value):
    high = lax.reduce_precision(value, exponent_bits=8, mantissa_bits=7)
    rest = value - high
    middle = lax.reduce_precision(rest, exponent_bits=8, mantissa_bits=7)
    return jnp.concatenate([high, middle, rest - middle])


def join_parts(parts):
    third = parts.shape[0] // 3
    parts = parts.astype(F32)
    return (parts[:third] + parts[third : 2 * third]) + parts[2 * third :]


def rows_of(flat, width):
    tile = 16 * width
    padded = -(-flat.shape[0] // tile) * tile
    return jnp.pad(flat, (0, padded - flat.shape[0])).reshape(-1, width).astype(BF16)


def on_device_body(
    light_query,
    light_key,
    light_value,
    light_gate,
    log_decay,
    norm_gain,
    soft_query,
    soft_key,
    soft_value,
    segment_ids,
):
    tok_rows = light_query.shape[0]
    heads_here = log_decay.shape[0]
    head_size = light_query.shape[1] // heads_here
    kv_here = soft_key.shape[1] // head_size
    assert -(-MAXDOC // tok_rows) == 4
    code = segment_ids.astype(F32) + 1.0
    decay_sum = jnp.cumsum(log_decay, axis=1)

    own_state = local_state_of(decay_sum, code, light_key, light_value)
    mixed = intra_mixed(decay_sum, code, light_query, light_key, light_value)
    block_decay = jnp.exp(decay_sum[:, -1])

    own_keys = soft_key.reshape(tok_rows, kv_here, head_size).transpose(1, 0, 2)
    own_values = soft_value.reshape(tok_rows, kv_here, head_size).transpose(1, 0, 2)
    kv_rows = kv_here * tok_rows
    own_kv = jnp.concatenate(
        [
            own_keys.reshape(kv_rows, head_size),
            own_values.reshape(kv_rows, head_size),
            rows_of(jnp.concatenate([code, split_parts(block_decay)]), head_size),
        ]
    )
    state_1, kv_1 = shifted((own_state, own_kv), "ctx", 1)
    state_2, kv_2 = shifted((own_state, own_kv), "ctx", 2)

    def unpack(block):
        keys = block[:kv_rows].reshape(kv_here, tok_rows, head_size)
        values = block[kv_rows : 2 * kv_rows].reshape(kv_here, tok_rows, head_size)
        meta = block[2 * kv_rows :].reshape(-1)
        codes = meta[:tok_rows].astype(F32)
        decay = join_parts(meta[tok_rows : tok_rows + 3 * heads_here])
        return keys, values, codes, decay

    keys_1, values_1, code_1, decay_1 = unpack(kv_1)
    keys_2, values_2, code_2, decay_2 = unpack(kv_2)

    link_1 = (code_2[-1] == code_1[0]) & (code_1[0] == code_1[-1])
    pair_state = state_1.astype(F32) + jnp.where(link_1, decay_1, 0.0)[:, None, None] * state_2.astype(F32)

    relay_kv = jnp.concatenate([kv_2[: 2 * kv_rows], kv_1[: 2 * kv_rows], rows_of(jnp.concatenate([code_2, code_1]), head_size)])
    state_far = shifted(pair_state.astype(BF16), "ctx", 2)
    kv_far = shifted(relay_kv, "ctx", 2)
    keys_4 = kv_far[:kv_rows].reshape(kv_here, tok_rows, head_size)
    values_4 = kv_far[kv_rows : 2 * kv_rows].reshape(kv_here, tok_rows, head_size)
    keys_3 = kv_far[2 * kv_rows : 3 * kv_rows].reshape(kv_here, tok_rows, head_size)
    values_3 = kv_far[3 * kv_rows : 4 * kv_rows].reshape(kv_here, tok_rows, head_size)
    code_far = kv_far[4 * kv_rows :].reshape(-1)[: 2 * tok_rows].astype(F32)
    code_4, code_3 = code_far[:tok_rows], code_far[tok_rows:]

    link_2 = (code_3[-1] == code_2[0]) & (code_2[0] == code_1[-1])
    carry_scale = jnp.where(link_2, decay_2 * decay_1, 0.0)
    uses_state = code == code_1[-1]
    scale_in = jnp.where(uses_state[None, :], jnp.exp(decay_sum), 0.0)
    mixed, squares = final_mixed(carry_scale, scale_in, light_query, mixed, pair_state, state_far)
    mixed = mixed.reshape(tok_rows, heads_here, head_size)
    squares = lax.psum(squares[:, 0], "tensor")
    features = heads_here * head_size * lax.axis_size("tensor")
    inverse = lax.rsqrt(squares / features + 1e-06)
    gate_open = jax.nn.sigmoid(light_gate.astype(F32)).reshape(tok_rows, heads_here, head_size)
    normed = mixed * inverse[:, None, None] * norm_gain.reshape(heads_here, head_size) * gate_open
    light_out = normed.reshape(tok_rows, heads_here * head_size).astype(BF16)

    key_window = jnp.concatenate([keys_4, keys_3, keys_2, keys_1, own_keys], axis=1)
    value_window = jnp.concatenate([values_4, values_3, values_2, values_1, own_values], axis=1)
    code_window = jnp.concatenate([code_4, code_3, code_2, code_1, code])
    soft_out = soft_window(soft_query, key_window, value_window, code, code_window, heads_here)
    return (light_out, soft_out)


def solution(mesh):
    in_specs = (
        P(("groups", "ctx"), "tensor"),
        P(("groups", "ctx"), "tensor"),
        P(("groups", "ctx"), "tensor"),
        P(("groups", "ctx"), "tensor"),
        P("tensor", ("groups", "ctx")),
        P("tensor"),
        P(("groups", "ctx"), "tensor"),
        P(("groups", "ctx"), "tensor"),
        P(("groups", "ctx"), "tensor"),
        P(("groups", "ctx")),
    )
    out_specs = (P(("groups", "ctx"), "tensor"), P(("groups", "ctx"), "tensor"))
    return jax.shard_map(on_device_body, mesh=mesh, in_specs=in_specs, out_specs=out_specs, check_vma=False)
```

```python
import jax
import jax.numpy as jnp
from jax import lax
from jax.experimental import pallas as pl
from jax.experimental.pallas import tpu as pltpu
from jax.sharding import PartitionSpec as P


NEG_BIG = -1e30
MAXDOC = 512
F32 = jnp.float32
BF16 = jnp.bfloat16


def shifted(block, axis, distance):
    devices = lax.axis_size(axis)
    route = [(i, i + distance) for i in range(devices - distance)]
    return lax.ppermute(block, axis, route)


def state_kernel(decay_ref, code_ref, key_ref, value_ref, out_ref):
    heads_here, head_size = out_ref.shape[0], out_ref.shape[1]
    tok_rows = code_ref.shape[0]
    code = code_ref[...]
    same_end = code == code[tok_rows - 1 :, :]
    for head in range(heads_here):
        decay = decay_ref[:, head : head + 1]
        to_end = jnp.where(same_end, jnp.exp(decay[tok_rows - 1 :, :] - decay), 0.0)
        columns = slice(head * head_size, (head + 1) * head_size)
        weighted = (key_ref[:, columns].astype(F32) * to_end).T.astype(BF16)
        out_ref[head] = jnp.dot(weighted, value_ref[:, columns], preferred_element_type=F32).astype(BF16)


def local_state_of(decay_sum, code, light_key, light_value):
    heads_here = decay_sum.shape[0]
    head_size = light_key.shape[1] // heads_here
    tok_rows = light_key.shape[0]
    flops = 2 * heads_here * tok_rows * head_size * head_size
    return pl.pallas_call(
        state_kernel,
        out_shape=jax.ShapeDtypeStruct((heads_here, head_size, head_size), BF16),
        in_specs=[pl.BlockSpec(memory_space=pltpu.VMEM)] * 4,
        out_specs=pl.BlockSpec(memory_space=pltpu.VMEM),
        cost_estimate=pl.CostEstimate(flops=flops, bytes_accessed=3 * light_key.size, transcendentals=heads_here * tok_rows),
    )(decay_sum.T, code[:, None], light_key, light_value)


def intra_kernel(decay_ref, decay_t_ref, code_row_ref, code_col_ref, query_ref, key_ref, value_ref, out_ref):
    heads_here = decay_ref.shape[0]
    tok_rows = code_col_ref.shape[0]
    head_size = query_ref.shape[1] // heads_here
    rows = lax.broadcasted_iota(jnp.int32, (tok_rows, tok_rows), 0)
    cols = lax.broadcasted_iota(jnp.int32, (tok_rows, tok_rows), 1)
    allowed = (code_col_ref[...] == code_row_ref[...]) & (cols <= rows)
    for head in range(heads_here):
        columns = slice(head * head_size, (head + 1) * head_size)
        gap = jnp.where(allowed, decay_t_ref[:, head : head + 1] - decay_ref[head : head + 1, :], -jnp.inf)
        products = lax.dot_general(
            query_ref[:, columns], key_ref[:, columns], (((1,), (1,)), ((), ())), preferred_element_type=F32
        )
        weights = (products * jnp.exp(gap)).astype(BF16)
        out_ref[:, columns] = jnp.dot(weights, value_ref[:, columns], preferred_element_type=F32)


def intra_mixed(decay_sum, code, light_query, light_key, light_value):
    heads_here = decay_sum.shape[0]
    tok_rows, width = light_query.shape
    flops = 4 * tok_rows * tok_rows * width
    return pl.pallas_call(
        intra_kernel,
        out_shape=jax.ShapeDtypeStruct((tok_rows, width), F32),
        in_specs=[pl.BlockSpec(memory_space=pltpu.VMEM)] * 7,
        out_specs=pl.BlockSpec(memory_space=pltpu.VMEM),
        cost_estimate=pl.CostEstimate(flops=flops, bytes_accessed=10 * light_query.size, transcendentals=heads_here * tok_rows * tok_rows),
    )(decay_sum, decay_sum.T, code[None, :], code[:, None], light_query, light_key, light_value)


def final_kernel(carry_ref, scale_t_ref, query_ref, mixed_ref, pair_ref, far_ref, out_ref, squares_ref):
    heads_here, head_size = pair_ref.shape[0], pair_ref.shape[1]
    squares = jnp.zeros((query_ref.shape[0], 1), F32)
    for head in range(heads_here):
        columns = slice(head * head_size, (head + 1) * head_size)
        state = pair_ref[head] + carry_ref[head] * far_ref[head].astype(F32)
        carried = jnp.dot(
            query_ref[:, columns].astype(F32), state, precision=lax.Precision.HIGHEST, preferred_element_type=F32
        )
        total = mixed_ref[:, columns] + carried * scale_t_ref[:, head : head + 1]
        out_ref[:, columns] = total
        squares = squares + jnp.sum(total * total, axis=1, keepdims=True)
    squares_ref[...] = squares


def final_mixed(carry_scale, scale_in, light_query, mixed, pair_state, state_far):
    tok_rows, width = light_query.shape
    flops = 12 * tok_rows * width * pair_state.shape[1]
    return pl.pallas_call(
        final_kernel,
        out_shape=(jax.ShapeDtypeStruct((tok_rows, width), F32), jax.ShapeDtypeStruct((tok_rows, 1), F32)),
        in_specs=[pl.BlockSpec(memory_space=pltpu.SMEM)] + [pl.BlockSpec(memory_space=pltpu.VMEM)] * 5,
        out_specs=(pl.BlockSpec(memory_space=pltpu.VMEM), pl.BlockSpec(memory_space=pltpu.VMEM)),
        cost_estimate=pl.CostEstimate(flops=flops, bytes_accessed=4 * mixed.size * 3, transcendentals=0),
    )(carry_scale, scale_in.T, light_query, mixed, pair_state, state_far)


def soft_window(soft_query, key_heads, value_heads, code, code_window, heads_here):
    tok_rows = soft_query.shape[0]
    kv_here, span, head_size = key_heads.shape
    group = heads_here // kv_here
    queries = soft_query.reshape(tok_rows, kv_here, group, head_size)
    key_position = jnp.arange(span)
    query_position = jnp.arange(tok_rows) + (span - tok_rows)
    allowed = (code[:, None] == code_window[None, :]) & (key_position[None, :] <= query_position[:, None])
    scores = jnp.einsum("tkgd,ksd->kgts", queries, key_heads, preferred_element_type=F32) * head_size ** (-0.5)
    scores = jnp.where(allowed, scores, NEG_BIG)
    row_max = jnp.max(scores, axis=-1)
    prob_block = jnp.exp(scores - row_max[..., None])
    row_total = jnp.sum(prob_block, axis=-1)
    weighted = jnp.einsum("kgts,ksd->kgtd", prob_block.astype(BF16), value_heads, preferred_element_type=F32)
    output = (weighted / row_total[..., None]).transpose(2, 0, 1, 3).reshape(tok_rows, heads_here * head_size)
    return output.astype(BF16)


def split_parts(value):
    high = lax.reduce_precision(value, exponent_bits=8, mantissa_bits=7)
    rest = value - high
    middle = lax.reduce_precision(rest, exponent_bits=8, mantissa_bits=7)
    return jnp.concatenate([high, middle, rest - middle])


def join_parts(parts):
    third = parts.shape[0] // 3
    parts = parts.astype(F32)
    return (parts[:third] + parts[third : 2 * third]) + parts[2 * third :]


def rows_of(flat, width):
    tile = 16 * width
    padded = -(-flat.shape[0] // tile) * tile
    return jnp.pad(flat, (0, padded - flat.shape[0])).reshape(-1, width).astype(BF16)


def on_device_body(
    light_query,
    light_key,
    light_value,
    light_gate,
    log_decay,
    norm_gain,
    soft_query,
    soft_key,
    soft_value,
    segment_ids,
):
    tok_rows = light_query.shape[0]
    heads_here = log_decay.shape[0]
    head_size = light_query.shape[1] // heads_here
    kv_here = soft_key.shape[1] // head_size
    assert -(-MAXDOC // tok_rows) == 4
    code = segment_ids.astype(F32) + 1.0
    decay_sum = jnp.cumsum(log_decay, axis=1)

    own_state = local_state_of(decay_sum, code, light_key, light_value)
    mixed = intra_mixed(decay_sum, code, light_query, light_key, light_value)
    block_decay = jnp.exp(decay_sum[:, -1])

    own_keys = soft_key.reshape(tok_rows, kv_here, head_size).transpose(1, 0, 2)
    own_values = soft_value.reshape(tok_rows, kv_here, head_size).transpose(1, 0, 2)
    kv_rows = kv_here * tok_rows
    own_kv = jnp.concatenate(
        [
            own_keys.reshape(kv_rows, head_size),
            own_values.reshape(kv_rows, head_size),
            rows_of(jnp.concatenate([code, split_parts(block_decay)]), head_size),
        ]
    )
    state_1 = shifted(own_state, "ctx", 1)
    state_2 = shifted(own_state, "ctx", 2)
    kv_1 = shifted(own_kv, "ctx", 1)
    kv_2 = shifted(own_kv, "ctx", 2)
    kv_3 = shifted(own_kv, "ctx", 3)
    kv_4 = shifted(own_kv, "ctx", 4)

    def unpack(block):
        keys = block[:kv_rows].reshape(kv_here, tok_rows, head_size)
        values = block[kv_rows : 2 * kv_rows].reshape(kv_here, tok_rows, head_size)
        meta = block[2 * kv_rows :].reshape(-1)
        codes = meta[:tok_rows].astype(F32)
        decay = join_parts(meta[tok_rows : tok_rows + 3 * heads_here])
        return keys, values, codes, decay

    keys_1, values_1, code_1, decay_1 = unpack(kv_1)
    keys_2, values_2, code_2, decay_2 = unpack(kv_2)

    link_1 = (code_2[-1] == code_1[0]) & (code_1[0] == code_1[-1])
    pair_state = state_1.astype(F32) + jnp.where(link_1, decay_1, 0.0)[:, None, None] * state_2.astype(F32)

    state_far = shifted(pair_state.astype(BF16), "ctx", 2)
    keys_3, values_3, code_3, _ = unpack(kv_3)
    keys_4, values_4, code_4, _ = unpack(kv_4)

    link_2 = (code_3[-1] == code_2[0]) & (code_2[0] == code_1[-1])
    carry_scale = jnp.where(link_2, decay_2 * decay_1, 0.0)
    uses_state = code == code_1[-1]
    scale_in = jnp.where(uses_state[None, :], jnp.exp(decay_sum), 0.0)
    mixed, squares = final_mixed(carry_scale, scale_in, light_query, mixed, pair_state, state_far)
    mixed = mixed.reshape(tok_rows, heads_here, head_size)
    squares = lax.psum(squares[:, 0], "tensor")
    features = heads_here * head_size * lax.axis_size("tensor")
    inverse = lax.rsqrt(squares / features + 1e-06)
    gate_open = jax.nn.sigmoid(light_gate.astype(F32)).reshape(tok_rows, heads_here, head_size)
    normed = mixed * inverse[:, None, None] * norm_gain.reshape(heads_here, head_size) * gate_open
    light_out = normed.reshape(tok_rows, heads_here * head_size).astype(BF16)

    key_window = jnp.concatenate([keys_4, keys_3, keys_2, keys_1, own_keys], axis=1)
    value_window = jnp.concatenate([values_4, values_3, values_2, values_1, own_values], axis=1)
    code_window = jnp.concatenate([code_4, code_3, code_2, code_1, code])
    soft_out = soft_window(soft_query, key_window, value_window, code, code_window, heads_here)
    return (light_out, soft_out)


def solution(mesh):
    in_specs = (
        P(("groups", "ctx"), "tensor"),
        P(("groups", "ctx"), "tensor"),
        P(("groups", "ctx"), "tensor"),
        P(("groups", "ctx"), "tensor"),
        P("tensor", ("groups", "ctx")),
        P("tensor"),
        P(("groups", "ctx"), "tensor"),
        P(("groups", "ctx"), "tensor"),
        P(("groups", "ctx"), "tensor"),
        P(("groups", "ctx")),
    )
    out_specs = (P(("groups", "ctx"), "tensor"), P(("groups", "ctx"), "tensor"))
    return jax.shard_map(on_device_body, mesh=mesh, in_specs=in_specs, out_specs=out_specs, check_vma=False)
```

```python
import jax
import jax.numpy as jnp
from jax import lax
from jax.experimental import pallas as pl
from jax.experimental.pallas import tpu as pltpu
from jax.sharding import PartitionSpec as P


NEG_BIG = -1e30
MAXDOC = 512
F32 = jnp.float32
BF16 = jnp.bfloat16


def shifted(block, axis, distance):
    devices = lax.axis_size(axis)
    route = [(i, i + distance) for i in range(devices - distance)]
    return lax.ppermute(block, axis, route)


def state_kernel(decay_ref, code_ref, key_ref, value_ref, out_ref):
    heads_here, head_size = out_ref.shape[0], out_ref.shape[1]
    tok_rows = code_ref.shape[0]
    code = code_ref[...]
    same_end = code == code[tok_rows - 1 :, :]
    for head in range(heads_here):
        decay = decay_ref[:, head : head + 1]
        to_end = jnp.where(same_end, jnp.exp(decay[tok_rows - 1 :, :] - decay), 0.0)
        columns = slice(head * head_size, (head + 1) * head_size)
        weighted = (key_ref[:, columns].astype(F32) * to_end).T.astype(BF16)
        out_ref[head] = jnp.dot(weighted, value_ref[:, columns], preferred_element_type=F32).astype(BF16)


def local_state_of(decay_sum, code, light_key, light_value):
    heads_here = decay_sum.shape[0]
    head_size = light_key.shape[1] // heads_here
    tok_rows = light_key.shape[0]
    flops = 2 * heads_here * tok_rows * head_size * head_size
    return pl.pallas_call(
        state_kernel,
        out_shape=jax.ShapeDtypeStruct((heads_here, head_size, head_size), BF16),
        in_specs=[pl.BlockSpec(memory_space=pltpu.VMEM)] * 4,
        out_specs=pl.BlockSpec(memory_space=pltpu.VMEM),
        cost_estimate=pl.CostEstimate(flops=flops, bytes_accessed=3 * light_key.size, transcendentals=heads_here * tok_rows),
    )(decay_sum.T, code[:, None], light_key, light_value)


def intra_kernel(decay_ref, decay_t_ref, code_row_ref, code_col_ref, query_ref, key_ref, value_ref, out_ref):
    heads_here = decay_ref.shape[0]
    tok_rows = code_col_ref.shape[0]
    head_size = query_ref.shape[1] // heads_here
    rows = lax.broadcasted_iota(jnp.int32, (tok_rows, tok_rows), 0)
    cols = lax.broadcasted_iota(jnp.int32, (tok_rows, tok_rows), 1)
    allowed = (code_col_ref[...] == code_row_ref[...]) & (cols <= rows)
    for head in range(heads_here):
        columns = slice(head * head_size, (head + 1) * head_size)
        gap = jnp.where(allowed, decay_t_ref[:, head : head + 1] - decay_ref[head : head + 1, :], -jnp.inf)
        products = lax.dot_general(
            query_ref[:, columns], key_ref[:, columns], (((1,), (1,)), ((), ())), preferred_element_type=F32
        )
        weights = (products * jnp.exp(gap)).astype(BF16)
        out_ref[:, columns] = jnp.dot(weights, value_ref[:, columns], preferred_element_type=F32)


def intra_mixed(decay_sum, code, light_query, light_key, light_value):
    heads_here = decay_sum.shape[0]
    tok_rows, width = light_query.shape
    flops = 4 * tok_rows * tok_rows * width
    return pl.pallas_call(
        intra_kernel,
        out_shape=jax.ShapeDtypeStruct((tok_rows, width), F32),
        in_specs=[pl.BlockSpec(memory_space=pltpu.VMEM)] * 7,
        out_specs=pl.BlockSpec(memory_space=pltpu.VMEM),
        cost_estimate=pl.CostEstimate(flops=flops, bytes_accessed=10 * light_query.size, transcendentals=heads_here * tok_rows * tok_rows),
    )(decay_sum, decay_sum.T, code[None, :], code[:, None], light_query, light_key, light_value)


def final_kernel(carry_ref, scale_t_ref, query_ref, mixed_ref, pair_ref, far_ref, out_ref, squares_ref):
    heads_here, head_size = pair_ref.shape[0], pair_ref.shape[1]
    squares = jnp.zeros((query_ref.shape[0], 1), F32)
    for head in range(heads_here):
        columns = slice(head * head_size, (head + 1) * head_size)
        state = pair_ref[head] + carry_ref[head] * far_ref[head].astype(F32)
        carried = jnp.dot(
            query_ref[:, columns].astype(F32), state, precision=lax.Precision.HIGHEST, preferred_element_type=F32
        )
        total = mixed_ref[:, columns] + carried * scale_t_ref[:, head : head + 1]
        out_ref[:, columns] = total
        squares = squares + jnp.sum(total * total, axis=1, keepdims=True)
    squares_ref[...] = squares


def final_mixed(carry_scale, scale_in, light_query, mixed, pair_state, state_far):
    tok_rows, width = light_query.shape
    flops = 12 * tok_rows * width * pair_state.shape[1]
    return pl.pallas_call(
        final_kernel,
        out_shape=(jax.ShapeDtypeStruct((tok_rows, width), F32), jax.ShapeDtypeStruct((tok_rows, 1), F32)),
        in_specs=[pl.BlockSpec(memory_space=pltpu.SMEM)] + [pl.BlockSpec(memory_space=pltpu.VMEM)] * 5,
        out_specs=(pl.BlockSpec(memory_space=pltpu.VMEM), pl.BlockSpec(memory_space=pltpu.VMEM)),
        cost_estimate=pl.CostEstimate(flops=flops, bytes_accessed=4 * mixed.size * 3, transcendentals=0),
    )(carry_scale, scale_in.T, light_query, mixed, pair_state, state_far)


def soft_window(soft_query, key_heads, value_heads, code, code_window, heads_here):
    tok_rows = soft_query.shape[0]
    kv_here, span, head_size = key_heads.shape
    group = heads_here // kv_here
    queries = soft_query.reshape(tok_rows, kv_here, group, head_size)
    key_position = jnp.arange(span)
    query_position = jnp.arange(tok_rows) + (span - tok_rows)
    allowed = (code[:, None] == code_window[None, :]) & (key_position[None, :] <= query_position[:, None])
    scores = jnp.einsum("tkgd,ksd->kgts", queries, key_heads, preferred_element_type=F32) * head_size ** (-0.5)
    scores = jnp.where(allowed, scores, NEG_BIG)
    row_max = jnp.max(scores, axis=-1)
    prob_block = jnp.exp(scores - row_max[..., None])
    row_total = jnp.sum(prob_block, axis=-1)
    weighted = jnp.einsum("kgts,ksd->kgtd", prob_block.astype(BF16), value_heads, preferred_element_type=F32)
    output = (weighted / row_total[..., None]).transpose(2, 0, 1, 3).reshape(tok_rows, heads_here * head_size)
    return output.astype(BF16)


def split_parts(value):
    high = lax.reduce_precision(value, exponent_bits=8, mantissa_bits=7)
    rest = value - high
    middle = lax.reduce_precision(rest, exponent_bits=8, mantissa_bits=7)
    return jnp.concatenate([high, middle, rest - middle])


def join_parts(parts):
    third = parts.shape[0] // 3
    parts = parts.astype(F32)
    return (parts[:third] + parts[third : 2 * third]) + parts[2 * third :]


def rows_of(flat, width):
    tile = 16 * width
    padded = -(-flat.shape[0] // tile) * tile
    return jnp.pad(flat, (0, padded - flat.shape[0])).reshape(-1, width).astype(BF16)


def on_device_body(
    light_query,
    light_key,
    light_value,
    light_gate,
    log_decay,
    norm_gain,
    soft_query,
    soft_key,
    soft_value,
    segment_ids,
):
    tok_rows = light_query.shape[0]
    heads_here = log_decay.shape[0]
    head_size = light_query.shape[1] // heads_here
    kv_here = soft_key.shape[1] // head_size
    assert -(-MAXDOC // tok_rows) == 4
    code = segment_ids.astype(F32) + 1.0
    decay_sum = jnp.cumsum(log_decay, axis=1)

    own_state = local_state_of(decay_sum, code, light_key, light_value)
    mixed = intra_mixed(decay_sum, code, light_query, light_key, light_value)
    block_decay = jnp.exp(decay_sum[:, -1])

    own_keys = soft_key.reshape(tok_rows, kv_here, head_size).transpose(1, 0, 2)
    own_values = soft_value.reshape(tok_rows, kv_here, head_size).transpose(1, 0, 2)
    kv_rows = kv_here * tok_rows
    own_kv = jnp.concatenate(
        [
            own_keys.reshape(kv_rows, head_size),
            own_values.reshape(kv_rows, head_size),
            rows_of(jnp.concatenate([code, split_parts(block_decay)]), head_size),
        ]
    )
    state_1, kv_1 = shifted((own_state, own_kv), "ctx", 1)
    state_2, kv_2 = shifted((own_state, own_kv), "ctx", 2)

    def unpack(block):
        keys = block[:kv_rows].reshape(kv_here, tok_rows, head_size)
        values = block[kv_rows : 2 * kv_rows].reshape(kv_here, tok_rows, head_size)
        meta = block[2 * kv_rows :].reshape(-1)
        codes = meta[:tok_rows].astype(F32)
        decay = join_parts(meta[tok_rows : tok_rows + 3 * heads_here])
        return keys, values, codes, decay

    keys_1, values_1, code_1, decay_1 = unpack(kv_1)
    keys_2, values_2, code_2, decay_2 = unpack(kv_2)

    link_1 = (code_2[-1] == code_1[0]) & (code_1[0] == code_1[-1])
    pair_state = state_1.astype(F32) + jnp.where(link_1, decay_1, 0.0)[:, None, None] * state_2.astype(F32)
    pair_wire = pair_state.astype(BF16)

    relay_kv = jnp.concatenate([kv_2[: 2 * kv_rows], kv_1[: 2 * kv_rows], rows_of(jnp.concatenate([code_2, code_1]), head_size)])
    state_far = shifted(pair_wire, "ctx", 2)
    kv_far = shifted(relay_kv, "ctx", 2)
    keys_4 = kv_far[:kv_rows].reshape(kv_here, tok_rows, head_size)
    values_4 = kv_far[kv_rows : 2 * kv_rows].reshape(kv_here, tok_rows, head_size)
    keys_3 = kv_far[2 * kv_rows : 3 * kv_rows].reshape(kv_here, tok_rows, head_size)
    values_3 = kv_far[3 * kv_rows : 4 * kv_rows].reshape(kv_here, tok_rows, head_size)
    code_far = kv_far[4 * kv_rows :].reshape(-1)[: 2 * tok_rows].astype(F32)
    code_4, code_3 = code_far[:tok_rows], code_far[tok_rows:]

    link_2 = (code_3[-1] == code_2[0]) & (code_2[0] == code_1[-1])
    carry_scale = jnp.where(link_2, decay_2 * decay_1, 0.0)
    uses_state = code == code_1[-1]
    scale_in = jnp.where(uses_state[None, :], jnp.exp(decay_sum), 0.0)
    mixed, squares = final_mixed(carry_scale, scale_in, light_query, mixed, pair_state, state_far)
    mixed = mixed.reshape(tok_rows, heads_here, head_size)
    squares = squares[:, 0]
    if lax.axis_size("tensor") == 2:
        squares = squares + lax.ppermute(squares, "tensor", [(0, 1), (1, 0)])
    else:
        squares = lax.psum(squares, "tensor")
    features = heads_here * head_size * lax.axis_size("tensor")
    inverse = lax.rsqrt(squares / features + 1e-06)
    gate_open = jax.nn.sigmoid(light_gate.astype(F32)).reshape(tok_rows, heads_here, head_size)
    normed = mixed * inverse[:, None, None] * norm_gain.reshape(heads_here, head_size) * gate_open
    light_out = normed.reshape(tok_rows, heads_here * head_size).astype(BF16)

    key_window = jnp.concatenate([keys_4, keys_3, keys_2, keys_1, own_keys], axis=1)
    value_window = jnp.concatenate([values_4, values_3, values_2, values_1, own_values], axis=1)
    code_window = jnp.concatenate([code_4, code_3, code_2, code_1, code])
    soft_out = soft_window(soft_query, key_window, value_window, code, code_window, heads_here)
    return (light_out, soft_out)


def solution(mesh):
    in_specs = (
        P(("groups", "ctx"), "tensor"),
        P(("groups", "ctx"), "tensor"),
        P(("groups", "ctx"), "tensor"),
        P(("groups", "ctx"), "tensor"),
        P("tensor", ("groups", "ctx")),
        P("tensor"),
        P(("groups", "ctx"), "tensor"),
        P(("groups", "ctx"), "tensor"),
        P(("groups", "ctx"), "tensor"),
        P(("groups", "ctx")),
    )
    out_specs = (P(("groups", "ctx"), "tensor"), P(("groups", "ctx"), "tensor"))
    return jax.shard_map(on_device_body, mesh=mesh, in_specs=in_specs, out_specs=out_specs, check_vma=False)
```

```python
import jax
import jax.numpy as jnp
from jax import lax
from jax.experimental import pallas as pl
from jax.experimental.pallas import tpu as pltpu
from jax.sharding import PartitionSpec as P


NEG_BIG = -1e30
MAXDOC = 512
F32 = jnp.float32
BF16 = jnp.bfloat16


def shifted(block, axis, distance):
    devices = lax.axis_size(axis)
    route = [(i, i + distance) for i in range(devices - distance)]
    return lax.ppermute(block, axis, route)


def state_kernel(decay_ref, code_ref, key_ref, value_ref, out_ref):
    heads_here, head_size = out_ref.shape[0], out_ref.shape[1]
    tok_rows = code_ref.shape[0]
    code = code_ref[...]
    same_end = code == code[tok_rows - 1 :, :]
    for head in range(heads_here):
        decay = decay_ref[:, head : head + 1]
        to_end = jnp.where(same_end, jnp.exp(decay[tok_rows - 1 :, :] - decay), 0.0)
        columns = slice(head * head_size, (head + 1) * head_size)
        weighted = (key_ref[:, columns].astype(F32) * to_end).T.astype(BF16)
        out_ref[head] = jnp.dot(weighted, value_ref[:, columns], preferred_element_type=F32).astype(BF16)


def local_state_of(decay_sum, code, light_key, light_value):
    heads_here = decay_sum.shape[0]
    head_size = light_key.shape[1] // heads_here
    tok_rows = light_key.shape[0]
    flops = 2 * heads_here * tok_rows * head_size * head_size
    return pl.pallas_call(
        state_kernel,
        out_shape=jax.ShapeDtypeStruct((heads_here, head_size, head_size), BF16),
        in_specs=[pl.BlockSpec(memory_space=pltpu.VMEM)] * 4,
        out_specs=pl.BlockSpec(memory_space=pltpu.VMEM),
        cost_estimate=pl.CostEstimate(flops=flops, bytes_accessed=3 * light_key.size, transcendentals=heads_here * tok_rows),
    )(decay_sum.T, code[:, None], light_key, light_value)


def intra_kernel(decay_ref, decay_t_ref, code_row_ref, code_col_ref, query_ref, key_ref, value_ref, out_ref):
    heads_here = decay_ref.shape[0]
    tok_rows = code_col_ref.shape[0]
    head_size = query_ref.shape[1] // heads_here
    rows = lax.broadcasted_iota(jnp.int32, (tok_rows, tok_rows), 0)
    cols = lax.broadcasted_iota(jnp.int32, (tok_rows, tok_rows), 1)
    allowed = (code_col_ref[...] == code_row_ref[...]) & (cols <= rows)
    for head in range(heads_here):
        columns = slice(head * head_size, (head + 1) * head_size)
        gap = jnp.where(allowed, decay_t_ref[:, head : head + 1] - decay_ref[head : head + 1, :], -jnp.inf)
        products = lax.dot_general(
            query_ref[:, columns], key_ref[:, columns], (((1,), (1,)), ((), ())), preferred_element_type=F32
        )
        weights = (products * jnp.exp(gap)).astype(BF16)
        out_ref[:, columns] = jnp.dot(weights, value_ref[:, columns], preferred_element_type=F32)


def intra_mixed(decay_sum, code, light_query, light_key, light_value):
    heads_here = decay_sum.shape[0]
    tok_rows, width = light_query.shape
    flops = 4 * tok_rows * tok_rows * width
    return pl.pallas_call(
        intra_kernel,
        out_shape=jax.ShapeDtypeStruct((tok_rows, width), F32),
        in_specs=[pl.BlockSpec(memory_space=pltpu.VMEM)] * 7,
        out_specs=pl.BlockSpec(memory_space=pltpu.VMEM),
        cost_estimate=pl.CostEstimate(flops=flops, bytes_accessed=10 * light_query.size, transcendentals=heads_here * tok_rows * tok_rows),
    )(decay_sum, decay_sum.T, code[None, :], code[:, None], light_query, light_key, light_value)


def final_kernel(carry_ref, scale_t_ref, query_ref, mixed_ref, pair_ref, far_ref, out_ref, squares_ref):
    heads_here, head_size = pair_ref.shape[0], pair_ref.shape[1]
    squares = jnp.zeros((query_ref.shape[0], 1), F32)
    for head in range(heads_here):
        columns = slice(head * head_size, (head + 1) * head_size)
        state = pair_ref[head] + carry_ref[head] * far_ref[head].astype(F32)
        carried = jnp.dot(
            query_ref[:, columns].astype(F32), state, precision=lax.Precision.HIGHEST, preferred_element_type=F32
        )
        total = mixed_ref[:, columns] + carried * scale_t_ref[:, head : head + 1]
        out_ref[:, columns] = total
        squares = squares + jnp.sum(total * total, axis=1, keepdims=True)
    squares_ref[...] = squares


def final_mixed(carry_scale, scale_in, light_query, mixed, pair_state, state_far):
    tok_rows, width = light_query.shape
    flops = 12 * tok_rows * width * pair_state.shape[1]
    return pl.pallas_call(
        final_kernel,
        out_shape=(jax.ShapeDtypeStruct((tok_rows, width), F32), jax.ShapeDtypeStruct((tok_rows, 1), F32)),
        in_specs=[pl.BlockSpec(memory_space=pltpu.SMEM)] + [pl.BlockSpec(memory_space=pltpu.VMEM)] * 5,
        out_specs=(pl.BlockSpec(memory_space=pltpu.VMEM), pl.BlockSpec(memory_space=pltpu.VMEM)),
        cost_estimate=pl.CostEstimate(flops=flops, bytes_accessed=4 * mixed.size * 3, transcendentals=0),
    )(carry_scale, scale_in.T, light_query, mixed, pair_state, state_far)


def soft_window(soft_query, key_heads, value_heads, code, code_window, heads_here):
    tok_rows = soft_query.shape[0]
    kv_here, span, head_size = key_heads.shape
    group = heads_here // kv_here
    queries = soft_query.reshape(tok_rows, kv_here, group, head_size)
    key_position = jnp.arange(span)
    query_position = jnp.arange(tok_rows) + (span - tok_rows)
    allowed = (code[:, None] == code_window[None, :]) & (key_position[None, :] <= query_position[:, None])
    scores = jnp.einsum("tkgd,ksd->kgts", queries, key_heads, preferred_element_type=F32) * head_size ** (-0.5)
    scores = jnp.where(allowed, scores, NEG_BIG)
    row_max = jnp.max(scores, axis=-1)
    prob_block = jnp.exp(scores - row_max[..., None])
    row_total = jnp.sum(prob_block, axis=-1)
    weighted = jnp.einsum("kgts,ksd->kgtd", prob_block.astype(BF16), value_heads, preferred_element_type=F32)
    output = (weighted / row_total[..., None]).transpose(2, 0, 1, 3).reshape(tok_rows, heads_here * head_size)
    return output.astype(BF16)


def split_parts(value):
    high = lax.reduce_precision(value, exponent_bits=8, mantissa_bits=7)
    rest = value - high
    middle = lax.reduce_precision(rest, exponent_bits=8, mantissa_bits=7)
    return jnp.concatenate([high, middle, rest - middle])


def join_parts(parts):
    third = parts.shape[0] // 3
    parts = parts.astype(F32)
    return (parts[:third] + parts[third : 2 * third]) + parts[2 * third :]


def rows_of(flat, width):
    tile = 16 * width
    padded = -(-flat.shape[0] // tile) * tile
    return jnp.pad(flat, (0, padded - flat.shape[0])).reshape(-1, width).astype(BF16)


def on_device_body(
    light_query,
    light_key,
    light_value,
    light_gate,
    log_decay,
    norm_gain,
    soft_query,
    soft_key,
    soft_value,
    segment_ids,
):
    tok_rows = light_query.shape[0]
    heads_here = log_decay.shape[0]
    head_size = light_query.shape[1] // heads_here
    kv_here = soft_key.shape[1] // head_size
    assert -(-MAXDOC // tok_rows) == 4
    code = segment_ids.astype(F32) + 1.0
    decay_sum = jnp.cumsum(log_decay, axis=1)

    own_state = local_state_of(decay_sum, code, light_key, light_value)
    mixed = intra_mixed(decay_sum, code, light_query, light_key, light_value)
    block_decay = jnp.exp(decay_sum[:, -1])

    own_keys = soft_key.reshape(tok_rows, kv_here, head_size).transpose(1, 0, 2)
    own_values = soft_value.reshape(tok_rows, kv_here, head_size).transpose(1, 0, 2)
    kv_rows = kv_here * tok_rows
    own_kv = jnp.concatenate(
        [
            own_keys.reshape(kv_rows, head_size),
            own_values.reshape(kv_rows, head_size),
            rows_of(jnp.concatenate([code, split_parts(block_decay)]), head_size),
        ]
    )
    state_1 = shifted(own_state, "ctx", 1)
    state_2 = shifted(own_state, "ctx", 2)
    kv_1 = shifted(own_kv, "ctx", 1)
    kv_2 = shifted(own_kv, "ctx", 2)

    def unpack(block):
        keys = block[:kv_rows].reshape(kv_here, tok_rows, head_size)
        values = block[kv_rows : 2 * kv_rows].reshape(kv_here, tok_rows, head_size)
        meta = block[2 * kv_rows :].reshape(-1)
        codes = meta[:tok_rows].astype(F32)
        decay = join_parts(meta[tok_rows : tok_rows + 3 * heads_here])
        return keys, values, codes, decay

    keys_1, values_1, code_1, decay_1 = unpack(kv_1)
    keys_2, values_2, code_2, decay_2 = unpack(kv_2)

    link_1 = (code_2[-1] == code_1[0]) & (code_1[0] == code_1[-1])
    pair_state = state_1.astype(F32) + jnp.where(link_1, decay_1, 0.0)[:, None, None] * state_2.astype(F32)
    pair_wire = pair_state.astype(BF16)

    relay_kv = jnp.concatenate([kv_2[: 2 * kv_rows], kv_1[: 2 * kv_rows], rows_of(jnp.concatenate([code_2, code_1]), head_size)])
    state_far = shifted(pair_wire, "ctx", 2)
    kv_far = shifted(relay_kv, "ctx", 2)
    keys_4 = kv_far[:kv_rows].reshape(kv_here, tok_rows, head_size)
    values_4 = kv_far[kv_rows : 2 * kv_rows].reshape(kv_here, tok_rows, head_size)
    keys_3 = kv_far[2 * kv_rows : 3 * kv_rows].reshape(kv_here, tok_rows, head_size)
    values_3 = kv_far[3 * kv_rows : 4 * kv_rows].reshape(kv_here, tok_rows, head_size)
    code_far = kv_far[4 * kv_rows :].reshape(-1)[: 2 * tok_rows].astype(F32)
    code_4, code_3 = code_far[:tok_rows], code_far[tok_rows:]

    link_2 = (code_3[-1] == code_2[0]) & (code_2[0] == code_1[-1])
    carry_scale = jnp.where(link_2, decay_2 * decay_1, 0.0)
    uses_state = code == code_1[-1]
    scale_in = jnp.where(uses_state[None, :], jnp.exp(decay_sum), 0.0)
    mixed, squares = final_mixed(carry_scale, scale_in, light_query, mixed, pair_state, state_far)
    mixed = mixed.reshape(tok_rows, heads_here, head_size)
    squares = lax.psum(squares[:, 0], "tensor")
    features = heads_here * head_size * lax.axis_size("tensor")
    inverse = lax.rsqrt(squares / features + 1e-06)
    gate_open = jax.nn.sigmoid(light_gate.astype(F32)).reshape(tok_rows, heads_here, head_size)
    normed = mixed * inverse[:, None, None] * norm_gain.reshape(heads_here, head_size) * gate_open
    light_out = normed.reshape(tok_rows, heads_here * head_size).astype(BF16)

    key_window = jnp.concatenate([keys_4, keys_3, keys_2, keys_1, own_keys], axis=1)
    value_window = jnp.concatenate([values_4, values_3, values_2, values_1, own_values], axis=1)
    code_window = jnp.concatenate([code_4, code_3, code_2, code_1, code])
    soft_out = soft_window(soft_query, key_window, value_window, code, code_window, heads_here)
    return (light_out, soft_out)


def solution(mesh):
    in_specs = (
        P(("groups", "ctx"), "tensor"),
        P(("groups", "ctx"), "tensor"),
        P(("groups", "ctx"), "tensor"),
        P(("groups", "ctx"), "tensor"),
        P("tensor", ("groups", "ctx")),
        P("tensor"),
        P(("groups", "ctx"), "tensor"),
        P(("groups", "ctx"), "tensor"),
        P(("groups", "ctx"), "tensor"),
        P(("groups", "ctx")),
    )
    out_specs = (P(("groups", "ctx"), "tensor"), P(("groups", "ctx"), "tensor"))
    return jax.shard_map(on_device_body, mesh=mesh, in_specs=in_specs, out_specs=out_specs, check_vma=False)
```

```python
import jax
import jax.numpy as jnp
from jax import lax
from jax.experimental import pallas as pl
from jax.experimental.pallas import tpu as pltpu
from jax.sharding import PartitionSpec as P


NEG_BIG = -1e30
MAXDOC = 512
F32 = jnp.float32
BF16 = jnp.bfloat16


def shifted(block, axis, distance):
    devices = lax.axis_size(axis)
    route = [(i, i + distance) for i in range(devices - distance)]
    return lax.ppermute(block, axis, route)


def state_kernel(decay_ref, code_ref, key_ref, value_ref, out_ref):
    heads_here, head_size = out_ref.shape[0], out_ref.shape[1]
    tok_rows = code_ref.shape[0]
    code = code_ref[...]
    same_end = code == code[tok_rows - 1 :, :]
    for head in range(heads_here):
        decay = decay_ref[:, head : head + 1]
        to_end = jnp.where(same_end, jnp.exp(decay[tok_rows - 1 :, :] - decay), 0.0)
        columns = slice(head * head_size, (head + 1) * head_size)
        weighted = (key_ref[:, columns].astype(F32) * to_end).T.astype(BF16)
        out_ref[head] = jnp.dot(weighted, value_ref[:, columns], preferred_element_type=F32).astype(BF16)


def local_state_of(decay_sum, code, light_key, light_value):
    heads_here = decay_sum.shape[0]
    head_size = light_key.shape[1] // heads_here
    tok_rows = light_key.shape[0]
    flops = 2 * heads_here * tok_rows * head_size * head_size
    return pl.pallas_call(
        state_kernel,
        out_shape=jax.ShapeDtypeStruct((heads_here, head_size, head_size), BF16),
        in_specs=[pl.BlockSpec(memory_space=pltpu.VMEM)] * 4,
        out_specs=pl.BlockSpec(memory_space=pltpu.VMEM),
        cost_estimate=pl.CostEstimate(flops=flops, bytes_accessed=3 * light_key.size, transcendentals=heads_here * tok_rows),
    )(decay_sum.T, code[:, None], light_key, light_value)


def intra_kernel(decay_ref, decay_t_ref, code_row_ref, code_col_ref, query_ref, key_ref, value_ref, out_ref):
    heads_here = decay_ref.shape[0]
    tok_rows = code_col_ref.shape[0]
    head_size = query_ref.shape[1] // heads_here
    rows = lax.broadcasted_iota(jnp.int32, (tok_rows, tok_rows), 0)
    cols = lax.broadcasted_iota(jnp.int32, (tok_rows, tok_rows), 1)
    allowed = (code_col_ref[...] == code_row_ref[...]) & (cols <= rows)
    for head in range(heads_here):
        columns = slice(head * head_size, (head + 1) * head_size)
        gap = jnp.where(allowed, decay_t_ref[:, head : head + 1] - decay_ref[head : head + 1, :], -jnp.inf)
        products = lax.dot_general(
            query_ref[:, columns], key_ref[:, columns], (((1,), (1,)), ((), ())), preferred_element_type=F32
        )
        weights = (products * jnp.exp(gap)).astype(BF16)
        out_ref[:, columns] = jnp.dot(weights, value_ref[:, columns], preferred_element_type=F32)


def intra_mixed(decay_sum, code, light_query, light_key, light_value):
    heads_here = decay_sum.shape[0]
    tok_rows, width = light_query.shape
    flops = 4 * tok_rows * tok_rows * width
    return pl.pallas_call(
        intra_kernel,
        out_shape=jax.ShapeDtypeStruct((tok_rows, width), F32),
        in_specs=[pl.BlockSpec(memory_space=pltpu.VMEM)] * 7,
        out_specs=pl.BlockSpec(memory_space=pltpu.VMEM),
        cost_estimate=pl.CostEstimate(flops=flops, bytes_accessed=10 * light_query.size, transcendentals=heads_here * tok_rows * tok_rows),
    )(decay_sum, decay_sum.T, code[None, :], code[:, None], light_query, light_key, light_value)


def final_kernel(carry_ref, scale_t_ref, query_ref, mixed_ref, pair_ref, far_ref, out_ref, squares_ref):
    heads_here, head_size = pair_ref.shape[0], pair_ref.shape[1]
    squares = jnp.zeros((query_ref.shape[0], 1), F32)
    for head in range(heads_here):
        columns = slice(head * head_size, (head + 1) * head_size)
        state = pair_ref[head] + carry_ref[head] * far_ref[head].astype(F32)
        query = query_ref[:, columns]
        high = state.astype(BF16)
        rest = state - high.astype(F32)
        middle = rest.astype(BF16)
        low = (rest - middle.astype(F32)).astype(BF16)
        carried = jnp.dot(query, high, preferred_element_type=F32)
        carried = carried + jnp.dot(query, middle, preferred_element_type=F32)
        carried = carried + jnp.dot(query, low, preferred_element_type=F32)
        total = mixed_ref[:, columns] + carried * scale_t_ref[:, head : head + 1]
        out_ref[:, columns] = total
        squares = squares + jnp.sum(total * total, axis=1, keepdims=True)
    squares_ref[...] = squares


def final_mixed(carry_scale, scale_in, light_query, mixed, pair_state, state_far):
    tok_rows, width = light_query.shape
    flops = 12 * tok_rows * width * pair_state.shape[1]
    return pl.pallas_call(
        final_kernel,
        out_shape=(jax.ShapeDtypeStruct((tok_rows, width), F32), jax.ShapeDtypeStruct((tok_rows, 1), F32)),
        in_specs=[pl.BlockSpec(memory_space=pltpu.SMEM)] + [pl.BlockSpec(memory_space=pltpu.VMEM)] * 5,
        out_specs=(pl.BlockSpec(memory_space=pltpu.VMEM), pl.BlockSpec(memory_space=pltpu.VMEM)),
        cost_estimate=pl.CostEstimate(flops=flops, bytes_accessed=4 * mixed.size * 3, transcendentals=0),
    )(carry_scale, scale_in.T, light_query, mixed, pair_state, state_far)


def soft_window(soft_query, key_heads, value_heads, code, code_window, heads_here):
    tok_rows = soft_query.shape[0]
    kv_here, span, head_size = key_heads.shape
    group = heads_here // kv_here
    queries = soft_query.reshape(tok_rows, kv_here, group, head_size)
    key_position = jnp.arange(span)
    query_position = jnp.arange(tok_rows) + (span - tok_rows)
    allowed = (code[:, None] == code_window[None, :]) & (key_position[None, :] <= query_position[:, None])
    scores = jnp.einsum("tkgd,ksd->kgts", queries, key_heads, preferred_element_type=F32) * head_size ** (-0.5)
    scores = jnp.where(allowed, scores, NEG_BIG)
    row_max = jnp.max(scores, axis=-1)
    prob_block = jnp.exp(scores - row_max[..., None])
    row_total = jnp.sum(prob_block, axis=-1)
    weighted = jnp.einsum("kgts,ksd->kgtd", prob_block.astype(BF16), value_heads, preferred_element_type=F32)
    output = (weighted / row_total[..., None]).transpose(2, 0, 1, 3).reshape(tok_rows, heads_here * head_size)
    return output.astype(BF16)


def split_parts(value):
    high = lax.reduce_precision(value, exponent_bits=8, mantissa_bits=7)
    rest = value - high
    middle = lax.reduce_precision(rest, exponent_bits=8, mantissa_bits=7)
    return jnp.concatenate([high, middle, rest - middle])


def join_parts(parts):
    third = parts.shape[0] // 3
    parts = parts.astype(F32)
    return (parts[:third] + parts[third : 2 * third]) + parts[2 * third :]


def rows_of(flat, width):
    tile = 16 * width
    padded = -(-flat.shape[0] // tile) * tile
    return jnp.pad(flat, (0, padded - flat.shape[0])).reshape(-1, width).astype(BF16)


def on_device_body(
    light_query,
    light_key,
    light_value,
    light_gate,
    log_decay,
    norm_gain,
    soft_query,
    soft_key,
    soft_value,
    segment_ids,
):
    tok_rows = light_query.shape[0]
    heads_here = log_decay.shape[0]
    head_size = light_query.shape[1] // heads_here
    kv_here = soft_key.shape[1] // head_size
    assert -(-MAXDOC // tok_rows) == 4
    code = segment_ids.astype(F32) + 1.0
    decay_sum = jnp.cumsum(log_decay, axis=1)

    own_state = local_state_of(decay_sum, code, light_key, light_value)
    mixed = intra_mixed(decay_sum, code, light_query, light_key, light_value)
    block_decay = jnp.exp(decay_sum[:, -1])

    own_keys = soft_key.reshape(tok_rows, kv_here, head_size).transpose(1, 0, 2)
    own_values = soft_value.reshape(tok_rows, kv_here, head_size).transpose(1, 0, 2)
    kv_rows = kv_here * tok_rows
    own_kv = jnp.concatenate(
        [
            own_keys.reshape(kv_rows, head_size),
            own_values.reshape(kv_rows, head_size),
            rows_of(jnp.concatenate([code, split_parts(block_decay)]), head_size),
        ]
    )
    state_1, kv_1 = shifted((own_state, own_kv), "ctx", 1)
    state_2, kv_2 = shifted((own_state, own_kv), "ctx", 2)

    def unpack(block):
        keys = block[:kv_rows].reshape(kv_here, tok_rows, head_size)
        values = block[kv_rows : 2 * kv_rows].reshape(kv_here, tok_rows, head_size)
        meta = block[2 * kv_rows :].reshape(-1)
        codes = meta[:tok_rows].astype(F32)
        decay = join_parts(meta[tok_rows : tok_rows + 3 * heads_here])
        return keys, values, codes, decay

    keys_1, values_1, code_1, decay_1 = unpack(kv_1)
    keys_2, values_2, code_2, decay_2 = unpack(kv_2)

    link_1 = (code_2[-1] == code_1[0]) & (code_1[0] == code_1[-1])
    pair_state = state_1.astype(F32) + jnp.where(link_1, decay_1, 0.0)[:, None, None] * state_2.astype(F32)
    pair_wire = pair_state.astype(BF16)

    relay_kv = jnp.concatenate([kv_2[: 2 * kv_rows], kv_1[: 2 * kv_rows], rows_of(jnp.concatenate([code_2, code_1]), head_size)])
    state_far = shifted(pair_wire, "ctx", 2)
    kv_far = shifted(relay_kv, "ctx", 2)
    keys_4 = kv_far[:kv_rows].reshape(kv_here, tok_rows, head_size)
    values_4 = kv_far[kv_rows : 2 * kv_rows].reshape(kv_here, tok_rows, head_size)
    keys_3 = kv_far[2 * kv_rows : 3 * kv_rows].reshape(kv_here, tok_rows, head_size)
    values_3 = kv_far[3 * kv_rows : 4 * kv_rows].reshape(kv_here, tok_rows, head_size)
    code_far = kv_far[4 * kv_rows :].reshape(-1)[: 2 * tok_rows].astype(F32)
    code_4, code_3 = code_far[:tok_rows], code_far[tok_rows:]

    link_2 = (code_3[-1] == code_2[0]) & (code_2[0] == code_1[-1])
    carry_scale = jnp.where(link_2, decay_2 * decay_1, 0.0)
    uses_state = code == code_1[-1]
    scale_in = jnp.where(uses_state[None, :], jnp.exp(decay_sum), 0.0)
    mixed, squares = final_mixed(carry_scale, scale_in, light_query, mixed, pair_state, state_far)
    mixed = mixed.reshape(tok_rows, heads_here, head_size)
    squares = lax.psum(squares[:, 0], "tensor")
    features = heads_here * head_size * lax.axis_size("tensor")
    inverse = lax.rsqrt(squares / features + 1e-06)
    gate_open = jax.nn.sigmoid(light_gate.astype(F32)).reshape(tok_rows, heads_here, head_size)
    normed = mixed * inverse[:, None, None] * norm_gain.reshape(heads_here, head_size) * gate_open
    light_out = normed.reshape(tok_rows, heads_here * head_size).astype(BF16)

    key_window = jnp.concatenate([keys_4, keys_3, keys_2, keys_1, own_keys], axis=1)
    value_window = jnp.concatenate([values_4, values_3, values_2, values_1, own_values], axis=1)
    code_window = jnp.concatenate([code_4, code_3, code_2, code_1, code])
    soft_out = soft_window(soft_query, key_window, value_window, code, code_window, heads_here)
    return (light_out, soft_out)


def solution(mesh):
    in_specs = (
        P(("groups", "ctx"), "tensor"),
        P(("groups", "ctx"), "tensor"),
        P(("groups", "ctx"), "tensor"),
        P(("groups", "ctx"), "tensor"),
        P("tensor", ("groups", "ctx")),
        P("tensor"),
        P(("groups", "ctx"), "tensor"),
        P(("groups", "ctx"), "tensor"),
        P(("groups", "ctx"), "tensor"),
        P(("groups", "ctx")),
    )
    out_specs = (P(("groups", "ctx"), "tensor"), P(("groups", "ctx"), "tensor"))
    return jax.shard_map(on_device_body, mesh=mesh, in_specs=in_specs, out_specs=out_specs, check_vma=False)
```

```python
import jax
import jax.numpy as jnp
from jax import lax
from jax.experimental import pallas as pl
from jax.experimental.pallas import tpu as pltpu
from jax.sharding import PartitionSpec as P


NEG_BIG = -1e30
MAXDOC = 512
F32 = jnp.float32
BF16 = jnp.bfloat16


def shifted(block, axis, distance):
    devices = lax.axis_size(axis)
    route = [(i, i + distance) for i in range(devices - distance)]
    return lax.ppermute(block, axis, route)


def state_kernel(decay_ref, code_ref, key_ref, value_ref, out_ref):
    heads_here, head_size = out_ref.shape[0], out_ref.shape[1]
    tok_rows = code_ref.shape[0]
    code = code_ref[...]
    same_end = code == code[tok_rows - 1 :, :]
    for head in range(heads_here):
        decay = decay_ref[:, head : head + 1]
        to_end = jnp.where(same_end, jnp.exp(decay[tok_rows - 1 :, :] - decay), 0.0)
        columns = slice(head * head_size, (head + 1) * head_size)
        weighted = (key_ref[:, columns].astype(F32) * to_end).T.astype(BF16)
        out_ref[head] = jnp.dot(weighted, value_ref[:, columns], preferred_element_type=F32).astype(BF16)


def local_state_of(decay_sum, code, light_key, light_value):
    heads_here = decay_sum.shape[0]
    head_size = light_key.shape[1] // heads_here
    tok_rows = light_key.shape[0]
    flops = 2 * heads_here * tok_rows * head_size * head_size
    return pl.pallas_call(
        state_kernel,
        out_shape=jax.ShapeDtypeStruct((heads_here, head_size, head_size), BF16),
        in_specs=[pl.BlockSpec(memory_space=pltpu.VMEM)] * 4,
        out_specs=pl.BlockSpec(memory_space=pltpu.VMEM),
        cost_estimate=pl.CostEstimate(flops=flops, bytes_accessed=3 * light_key.size, transcendentals=heads_here * tok_rows),
    )(decay_sum.T, code[:, None], light_key, light_value)


def intra_kernel(decay_ref, decay_t_ref, code_row_ref, code_col_ref, query_ref, key_ref, value_ref, out_ref):
    heads_here = decay_ref.shape[0]
    tok_rows = code_col_ref.shape[0]
    head_size = query_ref.shape[1] // heads_here
    rows = lax.broadcasted_iota(jnp.int32, (tok_rows, tok_rows), 0)
    cols = lax.broadcasted_iota(jnp.int32, (tok_rows, tok_rows), 1)
    allowed = (code_col_ref[...] == code_row_ref[...]) & (cols <= rows)
    for head in range(heads_here):
        columns = slice(head * head_size, (head + 1) * head_size)
        gap = jnp.where(allowed, decay_t_ref[:, head : head + 1] - decay_ref[head : head + 1, :], -jnp.inf)
        products = lax.dot_general(
            query_ref[:, columns], key_ref[:, columns], (((1,), (1,)), ((), ())), preferred_element_type=F32
        )
        weights = (products * jnp.exp(gap)).astype(BF16)
        out_ref[:, columns] = jnp.dot(weights, value_ref[:, columns], preferred_element_type=F32)


def intra_mixed(decay_sum, code, light_query, light_key, light_value):
    heads_here = decay_sum.shape[0]
    tok_rows, width = light_query.shape
    flops = 4 * tok_rows * tok_rows * width
    return pl.pallas_call(
        intra_kernel,
        out_shape=jax.ShapeDtypeStruct((tok_rows, width), F32),
        in_specs=[pl.BlockSpec(memory_space=pltpu.VMEM)] * 7,
        out_specs=pl.BlockSpec(memory_space=pltpu.VMEM),
        cost_estimate=pl.CostEstimate(flops=flops, bytes_accessed=10 * light_query.size, transcendentals=heads_here * tok_rows * tok_rows),
    )(decay_sum, decay_sum.T, code[None, :], code[:, None], light_query, light_key, light_value)


def final_kernel(carry_ref, scale_t_ref, query_ref, mixed_ref, pair_ref, far_ref, out_ref, squares_ref):
    heads_here, head_size = pair_ref.shape[0], pair_ref.shape[1]
    squares = jnp.zeros((query_ref.shape[0], 1), F32)
    for head in range(heads_here):
        columns = slice(head * head_size, (head + 1) * head_size)
        state = pair_ref[head] + carry_ref[head] * far_ref[head].astype(F32)
        carried = jnp.dot(
            query_ref[:, columns].astype(F32), state, precision=lax.Precision.HIGHEST, preferred_element_type=F32
        )
        total = mixed_ref[:, columns] + carried * scale_t_ref[:, head : head + 1]
        out_ref[:, columns] = total
        squares = squares + jnp.sum(total * total, axis=1, keepdims=True)
    squares_ref[...] = squares


def final_mixed(carry_scale, scale_in, light_query, mixed, pair_state, state_far):
    tok_rows, width = light_query.shape
    flops = 12 * tok_rows * width * pair_state.shape[1]
    return pl.pallas_call(
        final_kernel,
        out_shape=(jax.ShapeDtypeStruct((tok_rows, width), F32), jax.ShapeDtypeStruct((tok_rows, 1), F32)),
        in_specs=[pl.BlockSpec(memory_space=pltpu.SMEM)] + [pl.BlockSpec(memory_space=pltpu.VMEM)] * 5,
        out_specs=(pl.BlockSpec(memory_space=pltpu.VMEM), pl.BlockSpec(memory_space=pltpu.VMEM)),
        cost_estimate=pl.CostEstimate(flops=flops, bytes_accessed=4 * mixed.size * 3, transcendentals=0),
    )(carry_scale, scale_in.T, light_query, mixed, pair_state, state_far)


def soft_window(soft_query, key_heads, value_heads, code, code_window, heads_here):
    tok_rows = soft_query.shape[0]
    kv_here, span, head_size = key_heads.shape
    group = heads_here // kv_here
    queries = soft_query.reshape(tok_rows, kv_here, group, head_size)
    key_position = jnp.arange(span)
    query_position = jnp.arange(tok_rows) + (span - tok_rows)
    allowed = (code[:, None] == code_window[None, :]) & (key_position[None, :] <= query_position[:, None])
    scores = jnp.einsum("tkgd,ksd->kgts", queries, key_heads, preferred_element_type=F32) * head_size ** (-0.5)
    scores = jnp.where(allowed, scores, NEG_BIG)
    row_max = jnp.max(scores, axis=-1)
    prob_block = jnp.exp(scores - row_max[..., None])
    row_total = jnp.sum(prob_block, axis=-1)
    weighted = jnp.einsum("kgts,ksd->kgtd", prob_block.astype(BF16), value_heads, preferred_element_type=F32)
    output = (weighted / row_total[..., None]).transpose(2, 0, 1, 3).reshape(tok_rows, heads_here * head_size)
    return output.astype(BF16)


def split_parts(value):
    high = lax.reduce_precision(value, exponent_bits=8, mantissa_bits=7)
    rest = value - high
    middle = lax.reduce_precision(rest, exponent_bits=8, mantissa_bits=7)
    return jnp.concatenate([high, middle, rest - middle])


def join_parts(parts):
    third = parts.shape[0] // 3
    parts = parts.astype(F32)
    return (parts[:third] + parts[third : 2 * third]) + parts[2 * third :]


def rows_of(flat, width):
    tile = 16 * width
    padded = -(-flat.shape[0] // tile) * tile
    return jnp.pad(flat, (0, padded - flat.shape[0])).reshape(-1, width).astype(BF16)


def on_device_body(
    light_query,
    light_key,
    light_value,
    light_gate,
    log_decay,
    norm_gain,
    soft_query,
    soft_key,
    soft_value,
    segment_ids,
):
    tok_rows = light_query.shape[0]
    heads_here = log_decay.shape[0]
    head_size = light_query.shape[1] // heads_here
    kv_here = soft_key.shape[1] // head_size
    assert -(-MAXDOC // tok_rows) == 4
    code = segment_ids.astype(F32) + 1.0
    decay_sum = jnp.cumsum(log_decay, axis=1)

    own_state = local_state_of(decay_sum, code, light_key, light_value)
    mixed = intra_mixed(decay_sum, code, light_query, light_key, light_value)
    block_decay = jnp.exp(decay_sum[:, -1])

    own_keys = soft_key.reshape(tok_rows, kv_here, head_size).transpose(1, 0, 2)
    own_values = soft_value.reshape(tok_rows, kv_here, head_size).transpose(1, 0, 2)
    kv_rows = kv_here * tok_rows
    own_kv = jnp.concatenate(
        [
            own_keys.reshape(kv_rows, head_size),
            own_values.reshape(kv_rows, head_size),
            rows_of(jnp.concatenate([code, split_parts(block_decay)]), head_size),
        ]
    )
    state_1, kv_1 = shifted((own_state, own_kv), "ctx", 1)
    state_2, kv_2 = shifted((own_state, own_kv), "ctx", 2)

    def unpack(block):
        keys = block[:kv_rows].reshape(kv_here, tok_rows, head_size)
        values = block[kv_rows : 2 * kv_rows].reshape(kv_here, tok_rows, head_size)
        meta = block[2 * kv_rows :].reshape(-1)
        codes = meta[:tok_rows].astype(F32)
        decay = join_parts(meta[tok_rows : tok_rows + 3 * heads_here])
        return keys, values, codes, decay

    keys_1, values_1, code_1, decay_1 = unpack(kv_1)
    keys_2, values_2, code_2, decay_2 = unpack(kv_2)

    link_1 = (code_2[-1] == code_1[0]) & (code_1[0] == code_1[-1])
    pair_state = state_1.astype(F32) + jnp.where(link_1, decay_1, 0.0)[:, None, None] * state_2.astype(F32)
    pair_wire = pair_state.astype(BF16)

    relay_kv = jnp.concatenate([kv_2[: 2 * kv_rows], kv_1[: 2 * kv_rows], rows_of(jnp.concatenate([code_2, code_1]), head_size)])
    state_far = shifted(pair_wire, "ctx", 2)
    kv_far = shifted(relay_kv, "ctx", 2)
    keys_4 = kv_far[:kv_rows].reshape(kv_here, tok_rows, head_size)
    values_4 = kv_far[kv_rows : 2 * kv_rows].reshape(kv_here, tok_rows, head_size)
    keys_3 = kv_far[2 * kv_rows : 3 * kv_rows].reshape(kv_here, tok_rows, head_size)
    values_3 = kv_far[3 * kv_rows : 4 * kv_rows].reshape(kv_here, tok_rows, head_size)
    code_far = kv_far[4 * kv_rows :].reshape(-1)[: 2 * tok_rows].astype(F32)
    code_4, code_3 = code_far[:tok_rows], code_far[tok_rows:]

    link_2 = (code_3[-1] == code_2[0]) & (code_2[0] == code_1[-1])
    carry_scale = jnp.where(link_2, decay_2 * decay_1, 0.0)
    uses_state = code == code_1[-1]
    scale_in = jnp.where(uses_state[None, :], jnp.exp(decay_sum), 0.0)
    mixed, squares = final_mixed(carry_scale, scale_in, light_query, mixed, pair_state, state_far)
    mixed = mixed.reshape(tok_rows, heads_here, head_size)
    squares = lax.psum(squares, "tensor")
    features = heads_here * head_size * lax.axis_size("tensor")
    inverse = lax.rsqrt(squares / features + 1e-06)
    gate_open = jax.nn.sigmoid(light_gate.astype(F32)).reshape(tok_rows, heads_here, head_size)
    normed = mixed * inverse[:, :, None] * norm_gain.reshape(heads_here, head_size) * gate_open
    light_out = normed.reshape(tok_rows, heads_here * head_size).astype(BF16)

    key_window = jnp.concatenate([keys_4, keys_3, keys_2, keys_1, own_keys], axis=1)
    value_window = jnp.concatenate([values_4, values_3, values_2, values_1, own_values], axis=1)
    code_window = jnp.concatenate([code_4, code_3, code_2, code_1, code])
    soft_out = soft_window(soft_query, key_window, value_window, code, code_window, heads_here)
    return (light_out, soft_out)


def solution(mesh):
    in_specs = (
        P(("groups", "ctx"), "tensor"),
        P(("groups", "ctx"), "tensor"),
        P(("groups", "ctx"), "tensor"),
        P(("groups", "ctx"), "tensor"),
        P("tensor", ("groups", "ctx")),
        P("tensor"),
        P(("groups", "ctx"), "tensor"),
        P(("groups", "ctx"), "tensor"),
        P(("groups", "ctx"), "tensor"),
        P(("groups", "ctx")),
    )
    out_specs = (P(("groups", "ctx"), "tensor"), P(("groups", "ctx"), "tensor"))
    return jax.shard_map(on_device_body, mesh=mesh, in_specs=in_specs, out_specs=out_specs, check_vma=False)
```
